32 devices in a mesh: grp: 2 (over y), ctx: 8 (over z, x), head: 2 (over core).
Axes of the slice: x: 2, y: 2, z: 4, core: 2. Of those that a mesh axis runs over, the one named last changes fastest.
Arguments:
- queries: bfloat16 [2, 1024, 4096], P('grp', ('ctx', 'head')), parts along dimension 0, may hold values from -5.5 to 5.5
- key_states: bfloat16 [2, 1024, 1024], P('grp', ('ctx', 'head')), parts along dimension 0, may hold values from -5.5 to 5.5
- value_states: bfloat16 [2, 1024, 1024], P('grp', ('ctx', 'head')), parts along dimension 0, may hold values from -6 to 6
Outputs:
- attended: bfloat16 [2, 1024, 4096], P('grp', ('ctx', 'head')), parts along dimension 0
The draws below stay inside these ranges and needn't reach their ends.
There are 2 independent parts, one for each index of `grp`. The reference program is written for one: setup_inputs(seed, part) draws one part's arguments, and reference() takes and returns one part's arrays. A program takes and returns all parts, laid end to end along the dimension named above; each array names one. Nothing has to cross between parts.
All inputs are finite; a program needn't handle non-finite values.
Results may differ from the reference program's by a relative error of at most 0.004.
The reference program's roundings to bfloat16 on the way (of `right_rounded`, `key_mix`, `left_rounded`, `query_mix`, `final_left` and `value_mix`) count: a program that leaves them out, or rounds other values in their place, can miss the bound.
Values may be sent and summed in bfloat16 or wider, within the bound.
No kernel may reach another device: no remote copies, remote signals or barrier semaphores. Data moves between devices by JAX's collectives and lax.ppermute only.
A program may use at most 64 MiB of HBM per device.

```python
import math
import jax
import jax.numpy as jnp
from jax import lax

QH = 32
KVH = 8
DH = 128
SEQS = 1
BLEN = 128
BLOCKS = 8
LENGTH = 1024


def block_scales(key, salt):
    logs = jax.random.uniform(jax.random.fold_in(key, salt), (SEQS, BLOCKS, 1, 1, 1), jnp.float32, math.log(0.5), math.log(2.0))
    scales = jnp.broadcast_to(jnp.exp(logs), (SEQS, BLOCKS, BLEN, 1, 1))
    return scales.reshape(SEQS, LENGTH, 1, 1)


def draw_heads(key, heads, salt, scaled):
    if scaled:
        factor = block_scales(key, salt + 5)
    else:
        factor = jnp.ones((SEQS, LENGTH, 1, 1), jnp.float32)
    drawn = jax.random.normal(jax.random.fold_in(key, salt + 2), (SEQS, LENGTH, heads, DH), jnp.float32) * factor
    drawn = jnp.clip(drawn, -5.5, 5.5)
    return drawn.reshape(SEQS, LENGTH, heads * DH).astype(jnp.bfloat16)


def draw_queries(key, part):
    return draw_heads(key, QH, 11, False)


def draw_key_states(key, part):
    return draw_heads(key, KVH, 23, True)


def block_scale(rng, dims, split, smallest, largest):
    loudness = 1.0
    for dim, blocks in split:
        heights = jax.random.uniform(jax.random.fold_in(jax.random.fold_in(rng, 6), dim), (blocks,), jnp.float32, smallest / len(split), largest / len(split))
        loudness = loudness * jnp.repeat(jnp.exp(heights), dims[dim] // blocks).reshape((-1,) + (1,) * (len(dims) - 1 - dim))
    return loudness


def noise(stream_key, shape, scale, most, cuts=(), kind=jnp.bfloat16):
    values = jax.random.normal(stream_key, shape, jnp.float32) * scale
    if len(cuts) > 0:
        values = block_scale(stream_key, shape, cuts, -0.22, 0.18) * values
    return jnp.clip(values, min=-most, max=most).astype(kind)


def setup_inputs(seed: int = 0, part: int = 0) -> dict:
    seeds = jax.random.split(jax.random.key(seed), 4)
    part_keys = jax.random.split(jax.random.fold_in(seeds[3], part), 4)
    return {
        "queries": draw_queries(jax.random.fold_in(jax.random.fold_in(seeds[3], part), 71), part),
        "key_states": draw_key_states(jax.random.fold_in(jax.random.fold_in(seeds[3], part), 71), part),
        "value_states": noise(part_keys[2], (SEQS, LENGTH, KVH * DH), 1.0, 6.0, ((1, 16),)),
    }


def rounded_copy(tensor):
    return lax.optimization_barrier(tensor.astype(jnp.bfloat16)).astype(jnp.float32)

def right_step(logits, key_heads):
    weights = jax.nn.softmax(logits, axis=-1)
    entropy = jax.nn.logsumexp(logits, axis=-1) - lax.optimization_barrier(jnp.sum(weights * logits, axis=-1))
    rounded = rounded_copy(weights)
    key_mix = rounded_copy(jnp.einsum('ljgci,lijd->ljgcd', rounded, key_heads, precision=lax.Precision.HIGHEST))
    return (rounded, entropy, key_mix)

def left_step(query_heads, key_mix, entropy):
    logits = jnp.einsum('acjgd,ljgcd->cjgal', query_heads, key_mix, precision=lax.Precision.HIGHEST) / math.sqrt(DH)
    logits = logits + jnp.transpose(entropy, (3, 1, 2, 0))[:, :, :, None, :]
    weights = jax.nn.softmax(logits, axis=-1)
    return (weights, rounded_copy(weights))

def one_sequence(arrays):
    query_rows, key_rows, value_rows = arrays
    group_size = QH // KVH
    query_heads = query_rows.astype(jnp.float32).reshape(BLOCKS, BLEN, KVH, group_size, DH)
    key_heads = key_rows.astype(jnp.float32).reshape(BLOCKS, BLEN, KVH, DH)
    value_heads = value_rows.astype(jnp.float32).reshape(BLOCKS, BLEN, KVH, DH)
    first_logits = jnp.einsum('acjgd,aijd->ajgci', query_heads, key_heads, precision=lax.Precision.HIGHEST) / math.sqrt(DH)
    _, entropy, key_mix = right_step(first_logits, key_heads)
    weights, left_rounded = left_step(query_heads, key_mix, entropy)
    column_mass = jnp.transpose(lax.optimization_barrier(jnp.sum(weights, axis=3)), (3, 1, 2, 0))
    mixed_rows = jnp.einsum('cjgal,acjgd->ljgcd', left_rounded, query_heads, precision=lax.Precision.HIGHEST)
    query_mix = rounded_copy(mixed_rows / jnp.maximum(column_mass, 1.0)[..., None])
    second_logits = jnp.einsum('ljgcd,lijd->ljgci', query_mix, key_heads, precision=lax.Precision.HIGHEST) / math.sqrt(DH)
    right_rounded, entropy, key_mix = right_step(second_logits, key_heads)
    value_mix = rounded_copy(jnp.einsum('ljgci,lijd->ljgcd', right_rounded, value_heads, precision=lax.Precision.HIGHEST))
    _, final_left = left_step(query_heads, key_mix, entropy)
    attended = jnp.einsum('cjgal,ljgcd->acjgd', final_left, value_mix, precision=lax.Precision.HIGHEST)
    return attended.reshape(LENGTH, QH * DH).astype(jnp.bfloat16)

def reference(queries, key_states, value_states):
    return lax.map(one_sequence, (queries, key_states, value_states))
```

```python
import math

import jax
import jax.numpy as jnp
from jax import lax
from jax.sharding import PartitionSpec as P

DH = 128


def right_step(query_rows, key_heads, value_heads):
    seq_count, place_count, feature_width = query_rows.shape
    heads_kv = key_heads.shape[2]
    shaped = query_rows.reshape(seq_count, place_count, heads_kv, -1, DH)
    logits = jnp.einsum(
        "scjgd,sijd->sjgci", shaped, key_heads, preferred_element_type=jnp.float32
    ) / math.sqrt(DH)
    weights = jax.nn.softmax(logits, axis=-1)
    entropy = jax.nn.logsumexp(logits, axis=-1) - jnp.sum(weights * logits, axis=-1)
    rounded = weights.astype(jnp.bfloat16)
    key_mix = jnp.einsum(
        "sjgci,sijd->scjgd", rounded, key_heads, preferred_element_type=jnp.float32
    ).astype(jnp.bfloat16)
    entropy = jnp.transpose(entropy, (0, 3, 1, 2))
    value_mix = None
    if value_heads is not None:
        value_mix = jnp.einsum(
            "sjgci,sijd->scjgd", rounded, value_heads, preferred_element_type=jnp.float32
        ).astype(jnp.bfloat16)
        value_mix = value_mix.reshape(seq_count, place_count, feature_width)
    return key_mix.reshape(seq_count, place_count, feature_width), entropy, value_mix


def to_places(stacked, entropy, ctx):
    seq_count, place_count, kinds, feature_width = stacked.shape
    pairs = place_count * feature_width // DH
    chunk = pairs // ctx
    rows = jnp.moveaxis(stacked, 2, 1).reshape(seq_count, kinds, ctx, chunk, DH)
    rows = lax.all_to_all(rows, "ctx", split_axis=2, concat_axis=2, tiled=True)
    ent = entropy.reshape(seq_count, ctx, chunk)
    ent = lax.all_to_all(ent, "ctx", split_axis=1, concat_axis=1, tiled=True)
    return rows, ent


def to_blocks(grid, place_count, feature_width):
    seq_count = grid.shape[0]
    back = lax.all_to_all(grid, "ctx", split_axis=1, concat_axis=1, tiled=True)
    return back.reshape(seq_count, place_count, feature_width)


def left_step(query_grid, key_grid, entropy_grid):
    logits = jnp.einsum(
        "sapd,slpd->spal", query_grid, key_grid, preferred_element_type=jnp.float32
    ) / math.sqrt(DH)
    logits = logits + jnp.transpose(entropy_grid, (0, 2, 1))[:, :, None, :]
    weights = jax.nn.softmax(logits, axis=-1)
    return weights, weights.astype(jnp.bfloat16)


def make_local(ctx):
    def local(queries, key_states, value_states):
        seq_count, place_count, feature_width = queries.shape
        keys = lax.all_gather(key_states, "head", axis=1, tiled=True)
        values = lax.all_gather(value_states, "head", axis=1, tiled=True)
        block_len = keys.shape[1]
        heads_kv = keys.shape[2] // DH
        key_heads = keys.reshape(seq_count, block_len, heads_kv, DH)
        value_heads = values.reshape(seq_count, block_len, heads_kv, DH)

        key_mix, entropy, _ = right_step(queries, key_heads, None)
        stacked = jnp.stack([queries, key_mix], axis=2)
        rows, entropy_grid = to_places(stacked, entropy, ctx)
        query_grid, key_grid = rows[:, 0], rows[:, 1]

        weights, left_rounded = left_step(query_grid, key_grid, entropy_grid)
        column_mass = jnp.transpose(jnp.sum(weights, axis=2), (0, 2, 1))
        mixed = jnp.einsum(
            "spal,sapd->slpd", left_rounded, query_grid, preferred_element_type=jnp.float32
        )
        query_mix = (mixed / jnp.maximum(column_mass, 1.0)[..., None]).astype(jnp.bfloat16)
        returned = to_blocks(query_mix, place_count, feature_width)

        key_mix, entropy, value_mix = right_step(returned, key_heads, value_heads)
        stacked = jnp.stack([key_mix, value_mix], axis=2)
        rows, entropy_grid = to_places(stacked, entropy, ctx)
        key_grid, value_grid = rows[:, 0], rows[:, 1]

        _, final_left = left_step(query_grid, key_grid, entropy_grid)
        attended = jnp.einsum(
            "spal,slpd->sapd", final_left, value_grid, preferred_element_type=jnp.float32
        ).astype(jnp.bfloat16)
        return to_blocks(attended, place_count, feature_width)

    return local


def solution(mesh):
    placed = P("grp", ("ctx", "head"), None)
    return jax.shard_map(
        make_local(mesh.shape["ctx"]),
        mesh=mesh,
        in_specs=(placed, placed, placed),
        out_specs=placed,
        check_vma=False,
    )
```

```python
import math

import jax
import jax.numpy as jnp
from jax import lax
from jax.sharding import PartitionSpec as P

DH = 128


def right_step(query_rows, key_heads, value_heads):
    seq_count, place_count, feature_width = query_rows.shape
    heads_kv = key_heads.shape[2]
    shaped = query_rows.reshape(seq_count, place_count, heads_kv, -1, DH)
    logits = jnp.einsum(
        "scjgd,sijd->sjgci", shaped, key_heads, preferred_element_type=jnp.float32
    ) / math.sqrt(DH)
    weights = jax.nn.softmax(logits, axis=-1)
    entropy = jax.nn.logsumexp(logits, axis=-1) - jnp.sum(weights * logits, axis=-1)
    rounded = weights.astype(jnp.bfloat16)
    key_mix = jnp.einsum(
        "sjgci,sijd->scjgd", rounded, key_heads, preferred_element_type=jnp.float32
    ).astype(jnp.bfloat16)
    entropy = jnp.transpose(entropy, (0, 3, 1, 2))
    value_mix = None
    if value_heads is not None:
        value_mix = jnp.einsum(
            "sjgci,sijd->scjgd", rounded, value_heads, preferred_element_type=jnp.float32
        ).astype(jnp.bfloat16)
        value_mix = value_mix.reshape(seq_count, place_count, feature_width)
    return key_mix.reshape(seq_count, place_count, feature_width), entropy, value_mix


def entropy_rows(entropy, ctx):
    seq_count = entropy.shape[0]
    flat = entropy.reshape(seq_count, ctx, -1)
    chunk = flat.shape[2]
    high = lax.optimization_barrier(flat.astype(jnp.bfloat16))
    rest = flat - high.astype(jnp.float32)
    middle = lax.optimization_barrier(rest.astype(jnp.bfloat16))
    low = (rest - middle.astype(jnp.float32)).astype(jnp.bfloat16)
    terms = jnp.concatenate([high, middle, low], axis=2)
    row_count = -(-3 * chunk // DH)
    terms = jnp.pad(terms, ((0, 0), (0, 0), (0, row_count * DH - 3 * chunk)))
    return terms.reshape(seq_count, ctx, row_count, DH)


def entropy_from_rows(rows, chunk):
    seq_count, ctx = rows.shape[:2]
    terms = rows.reshape(seq_count, ctx, -1)[:, :, : 3 * chunk].astype(jnp.float32)
    return (terms[:, :, :chunk] + terms[:, :, chunk : 2 * chunk]) + terms[:, :, 2 * chunk :]


def pair_rows(rows, ctx):
    seq_count = rows.shape[0]
    return rows.reshape(seq_count, ctx, -1, DH)


def exchange(grid):
    return lax.all_to_all(grid, "ctx", split_axis=1, concat_axis=1, tiled=True)


def to_blocks(grid, place_count, feature_width):
    seq_count = grid.shape[0]
    return exchange(grid).reshape(seq_count, place_count, feature_width)


def left_step(query_grid, key_grid, entropy_grid):
    logits = jnp.einsum(
        "sapd,slpd->spal", query_grid, key_grid, preferred_element_type=jnp.float32
    ) / math.sqrt(DH)
    logits = logits + jnp.transpose(entropy_grid, (0, 2, 1))[:, :, None, :]
    weights = jax.nn.softmax(logits, axis=-1)
    return weights, weights.astype(jnp.bfloat16)


def make_local(ctx):
    def local(queries, key_states, value_states):
        seq_count, place_count, feature_width = queries.shape
        keys = lax.all_gather(key_states, "head", axis=1, tiled=True)
        values = lax.all_gather(value_states, "head", axis=1, tiled=True)
        block_len = keys.shape[1]
        heads_kv = keys.shape[2] // DH
        key_heads = keys.reshape(seq_count, block_len, heads_kv, DH)
        value_heads = values.reshape(seq_count, block_len, heads_kv, DH)

        key_mix, entropy, _ = right_step(queries, key_heads, None)
        query_rows = pair_rows(queries, ctx)
        chunk = query_rows.shape[2]
        rows = exchange(
            jnp.concatenate(
                [query_rows, pair_rows(key_mix, ctx), entropy_rows(entropy, ctx)], axis=2
            )
        )
        query_grid, key_grid = rows[:, :, :chunk], rows[:, :, chunk : 2 * chunk]
        entropy_grid = entropy_from_rows(rows[:, :, 2 * chunk :], chunk)

        weights, left_rounded = left_step(query_grid, key_grid, entropy_grid)
        column_mass = jnp.transpose(jnp.sum(weights, axis=2), (0, 2, 1))
        mixed = jnp.einsum(
            "spal,sapd->slpd", left_rounded, query_grid, preferred_element_type=jnp.float32
        )
        query_mix = (mixed / jnp.maximum(column_mass, 1.0)[..., None]).astype(jnp.bfloat16)
        returned = to_blocks(query_mix, place_count, feature_width)

        key_mix, entropy, value_mix = right_step(returned, key_heads, value_heads)
        rows = exchange(
            jnp.concatenate(
                [pair_rows(key_mix, ctx), pair_rows(value_mix, ctx), entropy_rows(entropy, ctx)],
                axis=2,
            )
        )
        key_grid, value_grid = rows[:, :, :chunk], rows[:, :, chunk : 2 * chunk]
        entropy_grid = entropy_from_rows(rows[:, :, 2 * chunk :], chunk)

        _, final_left = left_step(query_grid, key_grid, entropy_grid)
        attended = jnp.einsum(
            "spal,slpd->sapd", final_left, value_grid, preferred_element_type=jnp.float32
        ).astype(jnp.bfloat16)
        return to_blocks(attended, place_count, feature_width)

    return local


def solution(mesh):
    placed = P("grp", ("ctx", "head"), None)
    return jax.shard_map(
        make_local(mesh.shape["ctx"]),
        mesh=mesh,
        in_specs=(placed, placed, placed),
        out_specs=placed,
        check_vma=False,
    )
```

```python
import math

import jax
import jax.numpy as jnp
from jax import lax
from jax.sharding import PartitionSpec as P

DH = 128


def right_step(query_rows, key_heads, value_heads):
    seq_count, place_count, feature_width = query_rows.shape
    heads_kv = key_heads.shape[2]
    shaped = query_rows.reshape(seq_count, place_count, heads_kv, -1, DH)
    logits = jnp.einsum(
        "scjgd,sijd->sjgci", shaped, key_heads, preferred_element_type=jnp.float32
    ) / math.sqrt(DH)
    weights = jax.nn.softmax(logits, axis=-1)
    entropy = jax.nn.logsumexp(logits, axis=-1) - jnp.sum(weights * logits, axis=-1)
    rounded = weights.astype(jnp.bfloat16)
    key_mix = jnp.einsum(
        "sjgci,sijd->scjgd", rounded, key_heads, preferred_element_type=jnp.float32
    ).astype(jnp.bfloat16)
    entropy = jnp.transpose(entropy, (0, 3, 1, 2))
    value_mix = None
    if value_heads is not None:
        value_mix = jnp.einsum(
            "sjgci,sijd->scjgd", rounded, value_heads, preferred_element_type=jnp.float32
        ).astype(jnp.bfloat16)
        value_mix = value_mix.reshape(seq_count, place_count, feature_width)
    return key_mix.reshape(seq_count, place_count, feature_width), entropy, value_mix


def entropy_rows(entropy, ctx):
    seq_count = entropy.shape[0]
    flat = entropy.reshape(seq_count, ctx, -1)
    chunk = flat.shape[2]
    high = lax.optimization_barrier(flat.astype(jnp.bfloat16))
    rest = flat - high.astype(jnp.float32)
    middle = lax.optimization_barrier(rest.astype(jnp.bfloat16))
    low = (rest - middle.astype(jnp.float32)).astype(jnp.bfloat16)
    terms = jnp.concatenate([high, middle, low], axis=2)
    row_count = -(-3 * chunk // DH)
    terms = jnp.pad(terms, ((0, 0), (0, 0), (0, row_count * DH - 3 * chunk)))
    return terms.reshape(seq_count, ctx, row_count, DH)


def entropy_from_rows(rows, chunk):
    seq_count, ctx = rows.shape[:2]
    terms = rows.reshape(seq_count, ctx, -1)[:, :, : 3 * chunk].astype(jnp.float32)
    return (terms[:, :, :chunk] + terms[:, :, chunk : 2 * chunk]) + terms[:, :, 2 * chunk :]


def pair_rows(rows, ctx):
    seq_count = rows.shape[0]
    return rows.reshape(seq_count, ctx, -1, DH)


def exchange(grid):
    count = grid.shape[1]
    me = lax.axis_index("ctx")
    outgoing = jnp.roll(grid, -me, axis=1)
    pieces = [outgoing[:, 0]]
    for shift in range(1, count):
        pairs = [(src, (src + shift) % count) for src in range(count)]
        pieces.append(lax.ppermute(outgoing[:, shift], "ctx", pairs))
    ordered = jnp.stack([pieces[0]] + pieces[1:][::-1], axis=1)
    return jnp.roll(ordered, me, axis=1)


def to_blocks(grid, place_count, feature_width):
    seq_count = grid.shape[0]
    return exchange(grid).reshape(seq_count, place_count, feature_width)


def left_step(query_grid, key_grid, entropy_grid):
    logits = jnp.einsum(
        "sapd,slpd->spal", query_grid, key_grid, preferred_element_type=jnp.float32
    ) / math.sqrt(DH)
    logits = logits + jnp.transpose(entropy_grid, (0, 2, 1))[:, :, None, :]
    weights = jax.nn.softmax(logits, axis=-1)
    return weights, weights.astype(jnp.bfloat16)


def make_local(ctx):
    def local(queries, key_states, value_states):
        seq_count, place_count, feature_width = queries.shape
        keys = lax.all_gather(key_states, "head", axis=1, tiled=True)
        values = lax.all_gather(value_states, "head", axis=1, tiled=True)
        block_len = keys.shape[1]
        heads_kv = keys.shape[2] // DH
        key_heads = keys.reshape(seq_count, block_len, heads_kv, DH)
        value_heads = values.reshape(seq_count, block_len, heads_kv, DH)

        key_mix, entropy, _ = right_step(queries, key_heads, None)
        query_rows = pair_rows(queries, ctx)
        chunk = query_rows.shape[2]
        rows = exchange(
            jnp.concatenate(
                [query_rows, pair_rows(key_mix, ctx), entropy_rows(entropy, ctx)], axis=2
            )
        )
        query_grid, key_grid = rows[:, :, :chunk], rows[:, :, chunk : 2 * chunk]
        entropy_grid = entropy_from_rows(rows[:, :, 2 * chunk :], chunk)

        weights, left_rounded = left_step(query_grid, key_grid, entropy_grid)
        column_mass = jnp.transpose(jnp.sum(weights, axis=2), (0, 2, 1))
        mixed = jnp.einsum(
            "spal,sapd->slpd", left_rounded, query_grid, preferred_element_type=jnp.float32
        )
        query_mix = (mixed / jnp.maximum(column_mass, 1.0)[..., None]).astype(jnp.bfloat16)
        returned = to_blocks(query_mix, place_count, feature_width)

        key_mix, entropy, value_mix = right_step(returned, key_heads, value_heads)
        rows = exchange(
            jnp.concatenate(
                [pair_rows(key_mix, ctx), pair_rows(value_mix, ctx), entropy_rows(entropy, ctx)],
                axis=2,
            )
        )
        key_grid, value_grid = rows[:, :, :chunk], rows[:, :, chunk : 2 * chunk]
        entropy_grid = entropy_from_rows(rows[:, :, 2 * chunk :], chunk)

        _, final_left = left_step(query_grid, key_grid, entropy_grid)
        attended = jnp.einsum(
            "spal,slpd->sapd", final_left, value_grid, preferred_element_type=jnp.float32
        ).astype(jnp.bfloat16)
        return to_blocks(attended, place_count, feature_width)

    return local


def solution(mesh):
    placed = P("grp", ("ctx", "head"), None)
    return jax.shard_map(
        make_local(mesh.shape["ctx"]),
        mesh=mesh,
        in_specs=(placed, placed, placed),
        out_specs=placed,
        check_vma=False,
    )
```

```python
import math

import jax
import jax.numpy as jnp
from jax import lax
from jax.sharding import PartitionSpec as P

DH = 128


def right_step(query_rows, key_heads, value_heads):
    seq_count, place_count, feature_width = query_rows.shape
    heads_kv = key_heads.shape[2]
    shaped = query_rows.reshape(seq_count, place_count, heads_kv, -1, DH)
    logits = jnp.einsum(
        "scjgd,sijd->sjgci", shaped, key_heads, preferred_element_type=jnp.float32
    ) / math.sqrt(DH)
    weights = jax.nn.softmax(logits, axis=-1)
    entropy = jax.nn.logsumexp(logits, axis=-1) - jnp.sum(weights * logits, axis=-1)
    rounded = weights.astype(jnp.bfloat16)
    key_mix = jnp.einsum(
        "sjgci,sijd->scjgd", rounded, key_heads, preferred_element_type=jnp.float32
    ).astype(jnp.bfloat16)
    entropy = jnp.transpose(entropy, (0, 3, 1, 2))
    value_mix = None
    if value_heads is not None:
        value_mix = jnp.einsum(
            "sjgci,sijd->scjgd", rounded, value_heads, preferred_element_type=jnp.float32
        ).astype(jnp.bfloat16)
        value_mix = value_mix.reshape(seq_count, place_count, feature_width)
    return key_mix.reshape(seq_count, place_count, feature_width), entropy, value_mix


def entropy_rows(entropy, ctx):
    seq_count = entropy.shape[0]
    flat = entropy.reshape(seq_count, ctx, -1)
    chunk = flat.shape[2]
    high = lax.optimization_barrier(flat.astype(jnp.bfloat16))
    rest = flat - high.astype(jnp.float32)
    middle = lax.optimization_barrier(rest.astype(jnp.bfloat16))
    low = (rest - middle.astype(jnp.float32)).astype(jnp.bfloat16)
    terms = jnp.concatenate([high, middle, low], axis=2)
    row_count = -(-3 * chunk // DH)
    terms = jnp.pad(terms, ((0, 0), (0, 0), (0, row_count * DH - 3 * chunk)))
    return terms.reshape(seq_count, ctx, row_count, DH)


def entropy_from_rows(rows, chunk):
    seq_count, ctx = rows.shape[:2]
    terms = rows.reshape(seq_count, ctx, -1)[:, :, : 3 * chunk].astype(jnp.float32)
    return (terms[:, :, :chunk] + terms[:, :, chunk : 2 * chunk]) + terms[:, :, 2 * chunk :]


def pair_rows(rows, ctx):
    seq_count = rows.shape[0]
    return rows.reshape(seq_count, ctx, -1, DH)


def exchange(grid):
    return lax.all_to_all(grid, "ctx", split_axis=1, concat_axis=1, tiled=True)


def to_blocks(grid, place_count, feature_width):
    seq_count = grid.shape[0]
    return exchange(grid).reshape(seq_count, place_count, feature_width)


def left_step(query_grid, key_grid, entropy_grid):
    logits = jnp.einsum(
        "sapd,slpd->spal", query_grid, key_grid, preferred_element_type=jnp.float32
    ) / math.sqrt(DH)
    logits = logits + jnp.transpose(entropy_grid, (0, 2, 1))[:, :, None, :]
    weights = jax.nn.softmax(logits, axis=-1)
    return weights, weights.astype(jnp.bfloat16)


def make_local(ctx, streams):
    def local(queries, key_states, value_states):
        seq_count = queries.shape[0]
        keys = lax.all_gather(key_states, "head", axis=1, tiled=True)
        values = lax.all_gather(value_states, "head", axis=1, tiled=True)
        block_len = keys.shape[1]
        heads_kv = keys.shape[2] // DH
        key_heads = keys.reshape(seq_count, block_len, heads_kv, DH)
        value_heads = values.reshape(seq_count, block_len, heads_kv, DH)
        parts = jnp.split(queries, streams, axis=1)
        return jnp.concatenate(
            [pipeline(part, key_heads, value_heads, ctx) for part in parts], axis=1
        )

    return local


def pipeline(queries, key_heads, value_heads, ctx):
    seq_count, place_count, feature_width = queries.shape

    key_mix, entropy, _ = right_step(queries, key_heads, None)
    query_rows = pair_rows(queries, ctx)
    chunk = query_rows.shape[2]
    rows = exchange(
        jnp.concatenate(
            [query_rows, pair_rows(key_mix, ctx), entropy_rows(entropy, ctx)], axis=2
        )
    )
    query_grid, key_grid = rows[:, :, :chunk], rows[:, :, chunk : 2 * chunk]
    entropy_grid = entropy_from_rows(rows[:, :, 2 * chunk :], chunk)

    weights, left_rounded = left_step(query_grid, key_grid, entropy_grid)
    column_mass = jnp.transpose(jnp.sum(weights, axis=2), (0, 2, 1))
    mixed = jnp.einsum(
        "spal,sapd->slpd", left_rounded, query_grid, preferred_element_type=jnp.float32
    )
    query_mix = (mixed / jnp.maximum(column_mass, 1.0)[..., None]).astype(jnp.bfloat16)
    returned = to_blocks(query_mix, place_count, feature_width)

    key_mix, entropy, value_mix = right_step(returned, key_heads, value_heads)
    rows = exchange(
        jnp.concatenate(
            [pair_rows(key_mix, ctx), pair_rows(value_mix, ctx), entropy_rows(entropy, ctx)],
            axis=2,
        )
    )
    key_grid, value_grid = rows[:, :, :chunk], rows[:, :, chunk : 2 * chunk]
    entropy_grid = entropy_from_rows(rows[:, :, 2 * chunk :], chunk)

    _, final_left = left_step(query_grid, key_grid, entropy_grid)
    attended = jnp.einsum(
        "spal,slpd->sapd", final_left, value_grid, preferred_element_type=jnp.float32
    ).astype(jnp.bfloat16)
    return to_blocks(attended, place_count, feature_width)


def solution(mesh):
    placed = P("grp", ("ctx", "head"), None)
    return jax.shard_map(
        make_local(mesh.shape["ctx"], 2),
        mesh=mesh,
        in_specs=(placed, placed, placed),
        out_specs=placed,
        check_vma=False,
    )
```

```python
import math

import jax
import jax.numpy as jnp
from jax import lax
from jax.experimental import pallas as pl
from jax.sharding import PartitionSpec as P

DH = 128


def right_kernel(query_ref, key_ref, *refs):
    with_values = len(refs) == 4
    if with_values:
        value_ref, key_mix_ref, entropy_ref, value_mix_ref = refs
    else:
        key_mix_ref, entropy_ref = refs
    heads = query_ref.shape[1] // DH
    group = heads // (key_ref.shape[1] // DH)
    for head in range(heads):
        cols = slice(head * DH, (head + 1) * DH)
        kv_cols = slice((head // group) * DH, (head // group + 1) * DH)
        keys = key_ref[:, kv_cols]
        logits = lax.dot_general(
            query_ref[:, cols], keys, (((1,), (1,)), ((), ())),
            preferred_element_type=jnp.float32,
        ) / math.sqrt(DH)
        peak = jnp.max(logits, axis=1, keepdims=True)
        unnormalized = jnp.exp(logits - peak)
        total = jnp.sum(unnormalized, axis=1, keepdims=True)
        weights = unnormalized / total
        entropy = (jnp.log(total) + peak) - jnp.sum(weights * logits, axis=1, keepdims=True)
        entropy_ref[:, head : head + 1] = entropy
        rounded = weights.astype(jnp.bfloat16)
        key_mix_ref[:, cols] = jnp.dot(
            rounded, keys, preferred_element_type=jnp.float32
        ).astype(jnp.bfloat16)
        if with_values:
            value_mix_ref[:, cols] = jnp.dot(
                rounded, value_ref[:, kv_cols], preferred_element_type=jnp.float32
            ).astype(jnp.bfloat16)


def right_step(query_rows, keys, values):
    seq_count, place_count, feature_width = query_rows.shape
    heads = feature_width // DH
    row_spec = pl.BlockSpec((None, place_count, feature_width), lambda s: (s, 0, 0))
    kv_spec = pl.BlockSpec((None,) + keys.shape[1:], lambda s: (s, 0, 0))
    entropy_spec = pl.BlockSpec((None, place_count, heads), lambda s: (s, 0, 0))
    row_shape = jax.ShapeDtypeStruct(query_rows.shape, jnp.bfloat16)
    entropy_shape = jax.ShapeDtypeStruct((seq_count, place_count, heads), jnp.float32)
    if values is None:
        key_mix, entropy = pl.pallas_call(
            right_kernel,
            grid=(seq_count,),
            in_specs=[row_spec, kv_spec],
            out_specs=[row_spec, entropy_spec],
            out_shape=[row_shape, entropy_shape],
        )(query_rows, keys)
        return key_mix, entropy, None
    return pl.pallas_call(
        right_kernel,
        grid=(seq_count,),
        in_specs=[row_spec, kv_spec, kv_spec],
        out_specs=[row_spec, entropy_spec, row_spec],
        out_shape=[row_shape, entropy_shape, row_shape],
    )(query_rows, keys, values)


def entropy_rows(entropy, ctx):
    seq_count = entropy.shape[0]
    flat = entropy.reshape(seq_count, ctx, -1)
    chunk = flat.shape[2]
    high = lax.optimization_barrier(flat.astype(jnp.bfloat16))
    rest = flat - high.astype(jnp.float32)
    middle = lax.optimization_barrier(rest.astype(jnp.bfloat16))
    low = (rest - middle.astype(jnp.float32)).astype(jnp.bfloat16)
    terms = jnp.concatenate([high, middle, low], axis=2)
    row_count = -(-3 * chunk // DH)
    terms = jnp.pad(terms, ((0, 0), (0, 0), (0, row_count * DH - 3 * chunk)))
    return terms.reshape(seq_count, ctx, row_count, DH)


def entropy_from_rows(rows, chunk):
    seq_count, ctx = rows.shape[:2]
    terms = rows.reshape(seq_count, ctx, -1)[:, :, : 3 * chunk].astype(jnp.float32)
    return (terms[:, :, :chunk] + terms[:, :, chunk : 2 * chunk]) + terms[:, :, 2 * chunk :]


def pair_rows(rows, ctx):
    seq_count = rows.shape[0]
    return rows.reshape(seq_count, ctx, -1, DH)


def exchange(grid):
    return lax.all_to_all(grid, "ctx", split_axis=1, concat_axis=1, tiled=True)


def to_blocks(grid, place_count, feature_width):
    seq_count = grid.shape[0]
    return exchange(grid).reshape(seq_count, place_count, feature_width)


def left_step(query_grid, key_grid, entropy_grid):
    logits = jnp.einsum(
        "sapd,slpd->spal", query_grid, key_grid, preferred_element_type=jnp.float32
    ) / math.sqrt(DH)
    logits = logits + jnp.transpose(entropy_grid, (0, 2, 1))[:, :, None, :]
    weights = jax.nn.softmax(logits, axis=-1)
    return weights, weights.astype(jnp.bfloat16)


def make_local(ctx):
    def local(queries, key_states, value_states):
        seq_count, place_count, feature_width = queries.shape
        keys = lax.all_gather(key_states, "head", axis=1, tiled=True)
        values = lax.all_gather(value_states, "head", axis=1, tiled=True)
        key_heads, value_heads = keys, values

        key_mix, entropy, _ = right_step(queries, key_heads, None)
        query_rows = pair_rows(queries, ctx)
        chunk = query_rows.shape[2]
        rows = exchange(
            jnp.concatenate(
                [query_rows, pair_rows(key_mix, ctx), entropy_rows(entropy, ctx)], axis=2
            )
        )
        query_grid, key_grid = rows[:, :, :chunk], rows[:, :, chunk : 2 * chunk]
        entropy_grid = entropy_from_rows(rows[:, :, 2 * chunk :], chunk)

        weights, left_rounded = left_step(query_grid, key_grid, entropy_grid)
        column_mass = jnp.transpose(jnp.sum(weights, axis=2), (0, 2, 1))
        mixed = jnp.einsum(
            "spal,sapd->slpd", left_rounded, query_grid, preferred_element_type=jnp.float32
        )
        query_mix = (mixed / jnp.maximum(column_mass, 1.0)[..., None]).astype(jnp.bfloat16)
        returned = to_blocks(query_mix, place_count, feature_width)

        key_mix, entropy, value_mix = right_step(returned, key_heads, value_heads)
        rows = exchange(
            jnp.concatenate(
                [pair_rows(key_mix, ctx), pair_rows(value_mix, ctx), entropy_rows(entropy, ctx)],
                axis=2,
            )
        )
        key_grid, value_grid = rows[:, :, :chunk], rows[:, :, chunk : 2 * chunk]
        entropy_grid = entropy_from_rows(rows[:, :, 2 * chunk :], chunk)

        _, final_left = left_step(query_grid, key_grid, entropy_grid)
        attended = jnp.einsum(
            "spal,slpd->sapd", final_left, value_grid, preferred_element_type=jnp.float32
        ).astype(jnp.bfloat16)
        return to_blocks(attended, place_count, feature_width)

    return local


def solution(mesh):
    placed = P("grp", ("ctx", "head"), None)
    return jax.shard_map(
        make_local(mesh.shape["ctx"]),
        mesh=mesh,
        in_specs=(placed, placed, placed),
        out_specs=placed,
        check_vma=False,
    )
```

```python
import math

import jax
import jax.numpy as jnp
from jax import lax
from jax.sharding import PartitionSpec as P

DH = 128


def right_step(query_rows, key_heads, value_heads):
    seq_count, place_count, feature_width = query_rows.shape
    heads_kv = key_heads.shape[2]
    shaped = query_rows.reshape(seq_count, place_count, heads_kv, -1, DH)
    logits = jnp.einsum(
        "scjgd,sijd->sjgci", shaped, key_heads, preferred_element_type=jnp.float32
    ) / math.sqrt(DH)
    weights = jax.nn.softmax(logits, axis=-1)
    entropy = jax.nn.logsumexp(logits, axis=-1) - jnp.sum(weights * logits, axis=-1)
    rounded = weights.astype(jnp.bfloat16)
    key_mix = jnp.einsum(
        "sjgci,sijd->scjgd", rounded, key_heads, preferred_element_type=jnp.float32
    ).astype(jnp.bfloat16)
    entropy = jnp.transpose(entropy, (0, 3, 1, 2))
    value_mix = None
    if value_heads is not None:
        value_mix = jnp.einsum(
            "sjgci,sijd->scjgd", rounded, value_heads, preferred_element_type=jnp.float32
        ).astype(jnp.bfloat16)
        value_mix = value_mix.reshape(seq_count, place_count, feature_width)
    return key_mix.reshape(seq_count, place_count, feature_width), entropy, value_mix


def entropy_rows(entropy, ctx):
    seq_count = entropy.shape[0]
    flat = pair_entropy(entropy.reshape(seq_count, entropy.shape[1], -1), ctx)
    chunk = flat.shape[2]
    high = lax.optimization_barrier(flat.astype(jnp.bfloat16))
    rest = flat - high.astype(jnp.float32)
    middle = lax.optimization_barrier(rest.astype(jnp.bfloat16))
    low = (rest - middle.astype(jnp.float32)).astype(jnp.bfloat16)
    terms = jnp.concatenate([high, middle, low], axis=2)
    row_count = -(-3 * chunk // DH)
    terms = jnp.pad(terms, ((0, 0), (0, 0), (0, row_count * DH - 3 * chunk)))
    return terms.reshape(seq_count, ctx, row_count, DH)


def entropy_from_rows(rows, chunk):
    seq_count, ctx = rows.shape[:2]
    terms = rows.reshape(seq_count, ctx, -1)[:, :, : 3 * chunk].astype(jnp.float32)
    return (terms[:, :, :chunk] + terms[:, :, chunk : 2 * chunk]) + terms[:, :, 2 * chunk :]


def pair_rows(rows, ctx):
    seq_count, place_count, feature_width = rows.shape
    if place_count % ctx:
        return rows.reshape(seq_count, ctx, -1, DH)
    shaped = rows.reshape(seq_count, ctx, place_count // ctx, feature_width // DH, DH)
    return jnp.swapaxes(shaped, 2, 3).reshape(seq_count, ctx, -1, DH)


def rows_back(grid, place_count, feature_width):
    seq_count, ctx = grid.shape[:2]
    if place_count % ctx:
        return grid.reshape(seq_count, place_count, feature_width)
    shaped = grid.reshape(seq_count, ctx, feature_width // DH, place_count // ctx, DH)
    return jnp.swapaxes(shaped, 2, 3).reshape(seq_count, place_count, feature_width)


def pair_entropy(entropy, ctx):
    seq_count, place_count, heads = entropy.shape
    if place_count % ctx:
        return entropy.reshape(seq_count, ctx, -1)
    shaped = entropy.reshape(seq_count, ctx, place_count // ctx, heads)
    return jnp.swapaxes(shaped, 2, 3).reshape(seq_count, ctx, -1)


def exchange(grid):
    return lax.all_to_all(grid, "ctx", split_axis=1, concat_axis=1, tiled=True)


def to_blocks(grid, place_count, feature_width):
    return rows_back(exchange(grid), place_count, feature_width)


def left_step(query_grid, key_grid, entropy_grid):
    logits = jnp.einsum(
        "sapd,slpd->spal", query_grid, key_grid, preferred_element_type=jnp.float32
    ) / math.sqrt(DH)
    logits = logits + jnp.transpose(entropy_grid, (0, 2, 1))[:, :, None, :]
    weights = jax.nn.softmax(logits, axis=-1)
    return weights, weights.astype(jnp.bfloat16)


def make_local(ctx):
    def local(queries, key_states, value_states):
        seq_count, place_count, feature_width = queries.shape
        keys = lax.all_gather(key_states, "head", axis=1, tiled=True)
        values = lax.all_gather(value_states, "head", axis=1, tiled=True)
        block_len = keys.shape[1]
        heads_kv = keys.shape[2] // DH
        key_heads = keys.reshape(seq_count, block_len, heads_kv, DH)
        value_heads = values.reshape(seq_count, block_len, heads_kv, DH)

        key_mix, entropy, _ = right_step(queries, key_heads, None)
        query_rows = pair_rows(queries, ctx)
        chunk = query_rows.shape[2]
        rows = exchange(
            jnp.concatenate(
                [query_rows, pair_rows(key_mix, ctx), entropy_rows(entropy, ctx)], axis=2
            )
        )
        query_grid, key_grid = rows[:, :, :chunk], rows[:, :, chunk : 2 * chunk]
        entropy_grid = entropy_from_rows(rows[:, :, 2 * chunk :], chunk)

        weights, left_rounded = left_step(query_grid, key_grid, entropy_grid)
        column_mass = jnp.transpose(jnp.sum(weights, axis=2), (0, 2, 1))
        mixed = jnp.einsum(
            "spal,sapd->slpd", left_rounded, query_grid, preferred_element_type=jnp.float32
        )
        query_mix = (mixed / jnp.maximum(column_mass, 1.0)[..., None]).astype(jnp.bfloat16)
        returned = to_blocks(query_mix, place_count, feature_width)

        key_mix, entropy, value_mix = right_step(returned, key_heads, value_heads)
        rows = exchange(
            jnp.concatenate(
                [pair_rows(key_mix, ctx), pair_rows(value_mix, ctx), entropy_rows(entropy, ctx)],
                axis=2,
            )
        )
        key_grid, value_grid = rows[:, :, :chunk], rows[:, :, chunk : 2 * chunk]
        entropy_grid = entropy_from_rows(rows[:, :, 2 * chunk :], chunk)

        _, final_left = left_step(query_grid, key_grid, entropy_grid)
        attended = jnp.einsum(
            "spal,slpd->sapd", final_left, value_grid, preferred_element_type=jnp.float32
        ).astype(jnp.bfloat16)
        return to_blocks(attended, place_count, feature_width)

    return local


def solution(mesh):
    placed = P("grp", ("ctx", "head"), None)
    return jax.shard_map(
        make_local(mesh.shape["ctx"]),
        mesh=mesh,
        in_specs=(placed, placed, placed),
        out_specs=placed,
        check_vma=False,
    )
```

```python
import math

import jax
import jax.numpy as jnp
from jax import lax
from jax.sharding import PartitionSpec as P

DH = 128


def softmax_terms(logits):
    weights = jax.nn.softmax(logits, axis=-1)
    entropy = jax.nn.logsumexp(logits, axis=-1) - jnp.sum(weights * logits, axis=-1)
    return weights, entropy


def entropy_rows(flat):
    ctx, chunk = flat.shape
    high = lax.optimization_barrier(flat.astype(jnp.bfloat16))
    rest = flat - high.astype(jnp.float32)
    middle = lax.optimization_barrier(rest.astype(jnp.bfloat16))
    low = (rest - middle.astype(jnp.float32)).astype(jnp.bfloat16)
    terms = jnp.concatenate([high, middle, low], axis=1)
    row_count = -(-3 * chunk // DH)
    terms = jnp.pad(terms, ((0, 0), (0, row_count * DH - 3 * chunk)))
    return terms.reshape(ctx, row_count, DH)


def entropy_from_rows(rows, chunk):
    ctx = rows.shape[0]
    terms = rows.reshape(ctx, -1)[:, : 3 * chunk].astype(jnp.float32)
    return (terms[:, :chunk] + terms[:, chunk : 2 * chunk]) + terms[:, 2 * chunk :]


def exchange(grid):
    return lax.all_to_all(grid, "ctx", split_axis=0, concat_axis=0, tiled=True)


def left_step(query_grid, key_grid, entropy_grid):
    logits = jnp.einsum(
        "apd,lpd->pal", query_grid, key_grid, preferred_element_type=jnp.float32
    ) / math.sqrt(DH)
    logits = logits + jnp.transpose(entropy_grid, (1, 0))[:, None, :]
    weights = jax.nn.softmax(logits, axis=-1)
    return weights, weights.astype(jnp.bfloat16)


def to_dest(rows, ctx, heads_kv):
    place_count, group = rows.shape[0], rows.shape[2]
    repeat = ctx // heads_kv
    shaped = rows.reshape((repeat, place_count // repeat) + rows.shape[1:])
    shaped = jnp.moveaxis(shaped, 2, 0)
    return shaped.reshape((ctx, place_count // repeat * group) + rows.shape[3:])


def from_dest(grid, place_count, heads_kv):
    ctx = grid.shape[0]
    repeat = ctx // heads_kv
    shaped = grid.reshape(heads_kv, repeat, place_count // repeat, -1, DH)
    shaped = jnp.moveaxis(shaped, 0, 2)
    return shaped.reshape(place_count, -1)


def one_sequence(queries, keys, values, ctx):
    place_count, feature_width = queries.shape
    block_len = keys.shape[0]
    heads_kv = keys.shape[1] // DH
    repeat = ctx // heads_kv
    query_heads = queries.reshape(place_count, heads_kv, -1, DH)
    key_heads = keys.reshape(block_len, heads_kv, DH)
    value_heads = values.reshape(block_len, heads_kv, DH)

    logits = jnp.einsum(
        "cjgd,ijd->cjgi", query_heads, key_heads, preferred_element_type=jnp.float32
    ) / math.sqrt(DH)
    weights, entropy = softmax_terms(logits)
    rounded = weights.astype(jnp.bfloat16)
    key_mix = jnp.einsum(
        "cjgi,ijd->cjgd", rounded, key_heads, preferred_element_type=jnp.float32
    ).astype(jnp.bfloat16)

    query_rows = to_dest(query_heads, ctx, heads_kv)
    chunk = query_rows.shape[1]
    key_rows = jnp.repeat(jnp.swapaxes(key_heads, 0, 1), repeat, axis=0)
    value_rows = jnp.repeat(jnp.swapaxes(value_heads, 0, 1), repeat, axis=0)
    payload = jnp.concatenate(
        [
            query_rows,
            to_dest(key_mix, ctx, heads_kv),
            key_rows,
            value_rows,
            entropy_rows(to_dest(entropy, ctx, heads_kv)),
        ],
        axis=1,
    )
    rows = exchange(payload)
    query_grid = rows[:, :chunk]
    key_grid = rows[:, chunk : 2 * chunk]
    block_keys = rows[:, 2 * chunk : 2 * chunk + block_len]
    block_values = rows[:, 2 * chunk + block_len : 2 * chunk + 2 * block_len]
    entropy_grid = entropy_from_rows(rows[:, 2 * chunk + 2 * block_len :], chunk)

    weights, left_rounded = left_step(query_grid, key_grid, entropy_grid)
    column_mass = jnp.transpose(jnp.sum(weights, axis=1), (1, 0))
    mixed = jnp.einsum(
        "pal,apd->lpd", left_rounded, query_grid, preferred_element_type=jnp.float32
    )
    query_mix = (mixed / jnp.maximum(column_mass, 1.0)[..., None]).astype(jnp.bfloat16)

    logits = jnp.einsum(
        "lpd,lid->lpi", query_mix, block_keys, preferred_element_type=jnp.float32
    ) / math.sqrt(DH)
    weights, entropy = softmax_terms(logits)
    rounded = weights.astype(jnp.bfloat16)
    key_mix = jnp.einsum(
        "lpi,lid->lpd", rounded, block_keys, preferred_element_type=jnp.float32
    ).astype(jnp.bfloat16)
    value_mix = jnp.einsum(
        "lpi,lid->lpd", rounded, block_values, preferred_element_type=jnp.float32
    ).astype(jnp.bfloat16)

    _, final_left = left_step(query_grid, key_mix, entropy)
    attended = jnp.einsum(
        "pal,lpd->apd", final_left, value_mix, preferred_element_type=jnp.float32
    ).astype(jnp.bfloat16)
    return from_dest(exchange(attended), place_count, heads_kv)


def make_local(ctx):
    def local(queries, key_states, value_states):
        keys = lax.all_gather(key_states, "head", axis=1, tiled=True)
        values = lax.all_gather(value_states, "head", axis=1, tiled=True)
        return jnp.stack(
            [
                one_sequence(queries[s], keys[s], values[s], ctx)
                for s in range(queries.shape[0])
            ]
        )

    return local


def solution(mesh):
    placed = P("grp", ("ctx", "head"), None)
    return jax.shard_map(
        make_local(mesh.shape["ctx"]),
        mesh=mesh,
        in_specs=(placed, placed, placed),
        out_specs=placed,
        check_vma=False,
    )
```

```python
import math

import jax
import jax.numpy as jnp
from jax import lax
from jax.sharding import PartitionSpec as P

DH = 128


def softmax_terms(logits):
    weights = jax.nn.softmax(logits, axis=-1)
    entropy = jax.nn.logsumexp(logits, axis=-1) - jnp.sum(weights * logits, axis=-1)
    return weights, entropy


def entropy_rows(flat):
    ctx, chunk = flat.shape
    high = lax.optimization_barrier(flat.astype(jnp.bfloat16))
    rest = flat - high.astype(jnp.float32)
    middle = lax.optimization_barrier(rest.astype(jnp.bfloat16))
    low = (rest - middle.astype(jnp.float32)).astype(jnp.bfloat16)
    terms = jnp.concatenate([high, middle, low], axis=1)
    row_count = -(-3 * chunk // DH)
    terms = jnp.pad(terms, ((0, 0), (0, row_count * DH - 3 * chunk)))
    return terms.reshape(ctx, row_count, DH)


def entropy_from_rows(rows, chunk):
    ctx = rows.shape[0]
    terms = rows.reshape(ctx, -1)[:, : 3 * chunk].astype(jnp.float32)
    return (terms[:, :chunk] + terms[:, chunk : 2 * chunk]) + terms[:, 2 * chunk :]


def exchange(grid):
    return lax.all_to_all(grid, "ctx", split_axis=0, concat_axis=0, tiled=True)


def left_step(query_grid, key_grid, entropy_grid):
    logits = jnp.einsum(
        "apd,lpd->pal", query_grid, key_grid, preferred_element_type=jnp.float32
    ) / math.sqrt(DH)
    logits = logits + jnp.transpose(entropy_grid, (1, 0))[:, None, :]
    weights = jax.nn.softmax(logits, axis=-1)
    return weights, weights.astype(jnp.bfloat16)


def to_dest(rows, ctx, heads_kv):
    place_count, group = rows.shape[0], rows.shape[2]
    repeat = ctx // heads_kv
    shaped = rows.reshape((repeat, place_count // repeat) + rows.shape[1:])
    shaped = jnp.moveaxis(shaped, 2, 0)
    return shaped.reshape((ctx, place_count // repeat * group) + rows.shape[3:])


def from_dest(grid, place_count, heads_kv):
    ctx = grid.shape[0]
    repeat = ctx // heads_kv
    shaped = grid.reshape(heads_kv, repeat, place_count // repeat, -1, DH)
    shaped = jnp.moveaxis(shaped, 0, 2)
    return shaped.reshape(place_count, -1)


def one_sequence(queries, keys, values, ctx):
    place_count, feature_width = queries.shape
    block_len = keys.shape[0]
    heads_kv = keys.shape[1] // DH
    repeat = ctx // heads_kv
    query_heads = queries.reshape(place_count, heads_kv, -1, DH)
    key_heads = keys.reshape(block_len, heads_kv, DH)
    value_heads = values.reshape(block_len, heads_kv, DH)

    query_rows = to_dest(query_heads, ctx, heads_kv)
    chunk = query_rows.shape[1]
    by_head = query_rows.reshape(heads_kv, -1, DH)
    logits = jnp.einsum(
        "jpd,ijd->jpi", by_head, key_heads, preferred_element_type=jnp.float32
    ) / math.sqrt(DH)
    weights, entropy = softmax_terms(logits)
    rounded = weights.astype(jnp.bfloat16)
    key_mix = jnp.einsum(
        "jpi,ijd->jpd", rounded, key_heads, preferred_element_type=jnp.float32
    ).astype(jnp.bfloat16)

    key_rows = jnp.repeat(jnp.swapaxes(key_heads, 0, 1), repeat, axis=0)
    value_rows = jnp.repeat(jnp.swapaxes(value_heads, 0, 1), repeat, axis=0)
    payload = jnp.concatenate(
        [
            query_rows,
            key_mix.reshape(ctx, chunk, DH),
            key_rows,
            value_rows,
            entropy_rows(entropy.reshape(ctx, chunk)),
        ],
        axis=1,
    )
    rows = exchange(payload)
    query_grid = rows[:, :chunk]
    key_grid = rows[:, chunk : 2 * chunk]
    block_keys = rows[:, 2 * chunk : 2 * chunk + block_len]
    block_values = rows[:, 2 * chunk + block_len : 2 * chunk + 2 * block_len]
    entropy_grid = entropy_from_rows(rows[:, 2 * chunk + 2 * block_len :], chunk)

    weights, left_rounded = left_step(query_grid, key_grid, entropy_grid)
    column_mass = jnp.transpose(jnp.sum(weights, axis=1), (1, 0))
    mixed = jnp.einsum(
        "pal,apd->lpd", left_rounded, query_grid, preferred_element_type=jnp.float32
    )
    query_mix = (mixed / jnp.maximum(column_mass, 1.0)[..., None]).astype(jnp.bfloat16)

    logits = jnp.einsum(
        "lpd,lid->lpi", query_mix, block_keys, preferred_element_type=jnp.float32
    ) / math.sqrt(DH)
    weights, entropy = softmax_terms(logits)
    rounded = weights.astype(jnp.bfloat16)
    key_mix = jnp.einsum(
        "lpi,lid->lpd", rounded, block_keys, preferred_element_type=jnp.float32
    ).astype(jnp.bfloat16)
    value_mix = jnp.einsum(
        "lpi,lid->lpd", rounded, block_values, preferred_element_type=jnp.float32
    ).astype(jnp.bfloat16)

    _, final_left = left_step(query_grid, key_mix, entropy)
    attended = jnp.einsum(
        "pal,lpd->apd", final_left, value_mix, preferred_element_type=jnp.float32
    ).astype(jnp.bfloat16)
    return from_dest(exchange(attended), place_count, heads_kv)


def make_local(ctx):
    def local(queries, key_states, value_states):
        both = lax.all_gather(
            jnp.concatenate([key_states, value_states], axis=2), "head", axis=1, tiled=True
        )
        width = key_states.shape[2]
        keys, values = both[:, :, :width], both[:, :, width:]
        return jnp.stack(
            [
                one_sequence(queries[s], keys[s], values[s], ctx)
                for s in range(queries.shape[0])
            ]
        )

    return local


def solution(mesh):
    placed = P("grp", ("ctx", "head"), None)
    return jax.shard_map(
        make_local(mesh.shape["ctx"]),
        mesh=mesh,
        in_specs=(placed, placed, placed),
        out_specs=placed,
        check_vma=False,
    )
```

```python
import math

import jax
import jax.numpy as jnp
from jax import lax
from jax.sharding import PartitionSpec as P

DH = 128


def softmax_terms(logits):
    weights = jax.nn.softmax(logits, axis=-1)
    entropy = jax.nn.logsumexp(logits, axis=-1) - jnp.sum(weights * logits, axis=-1)
    return weights, entropy


def entropy_rows(flat):
    ctx, chunk = flat.shape
    high = lax.optimization_barrier(flat.astype(jnp.bfloat16))
    rest = flat - high.astype(jnp.float32)
    middle = lax.optimization_barrier(rest.astype(jnp.bfloat16))
    low = (rest - middle.astype(jnp.float32)).astype(jnp.bfloat16)
    terms = jnp.concatenate([high, middle, low], axis=1)
    row_count = -(-3 * chunk // DH)
    terms = jnp.pad(terms, ((0, 0), (0, row_count * DH - 3 * chunk)))
    return terms.reshape(ctx, row_count, DH)


def entropy_from_rows(rows, chunk):
    ctx = rows.shape[0]
    terms = rows.reshape(ctx, -1)[:, : 3 * chunk].astype(jnp.float32)
    return (terms[:, :chunk] + terms[:, chunk : 2 * chunk]) + terms[:, 2 * chunk :]


def exchange(grid):
    return lax.all_to_all(grid, "ctx", split_axis=0, concat_axis=0, tiled=True)


def left_step(query_grid, key_grid, entropy_grid):
    logits = jnp.einsum(
        "apd,lpd->pal", query_grid, key_grid, preferred_element_type=jnp.float32
    ) / math.sqrt(DH)
    logits = logits + jnp.transpose(entropy_grid, (1, 0))[:, None, :]
    weights = jax.nn.softmax(logits, axis=-1)
    return weights, weights.astype(jnp.bfloat16)


def to_dest(rows, ctx, heads_kv):
    place_count, group = rows.shape[0], rows.shape[2]
    repeat = ctx // heads_kv
    shaped = rows.reshape((repeat, place_count // repeat) + rows.shape[1:])
    shaped = jnp.moveaxis(shaped, 2, 0)
    return shaped.reshape((ctx, place_count // repeat * group) + rows.shape[3:])


def from_dest(grid, place_count, heads_kv):
    ctx = grid.shape[0]
    repeat = ctx // heads_kv
    shaped = grid.reshape(heads_kv, repeat, place_count // repeat, -1, DH)
    shaped = jnp.moveaxis(shaped, 0, 2)
    return shaped.reshape(place_count, -1)


def one_sequence(queries, keys, own_keys, own_values, ctx):
    place_count, feature_width = queries.shape
    block_len = keys.shape[0]
    heads_kv = keys.shape[1] // DH
    repeat = ctx // heads_kv
    query_heads = queries.reshape(place_count, heads_kv, -1, DH)
    key_heads = keys.reshape(block_len, heads_kv, DH)

    query_rows = to_dest(query_heads, ctx, heads_kv)
    chunk = query_rows.shape[1]
    by_head = query_rows.reshape(heads_kv, -1, DH)
    logits = jnp.einsum(
        "jpd,ijd->jpi", by_head, key_heads, preferred_element_type=jnp.float32
    ) / math.sqrt(DH)
    weights, entropy = softmax_terms(logits)
    rounded = weights.astype(jnp.bfloat16)
    key_mix = jnp.einsum(
        "jpi,ijd->jpd", rounded, key_heads, preferred_element_type=jnp.float32
    ).astype(jnp.bfloat16)

    own_len = own_keys.shape[0]
    key_rows = jnp.repeat(
        jnp.swapaxes(own_keys.reshape(own_len, heads_kv, DH), 0, 1), repeat, axis=0
    )
    value_rows = jnp.repeat(
        jnp.swapaxes(own_values.reshape(own_len, heads_kv, DH), 0, 1), repeat, axis=0
    )
    payload = jnp.concatenate(
        [
            query_rows,
            key_mix.reshape(ctx, chunk, DH),
            key_rows,
            value_rows,
            entropy_rows(entropy.reshape(ctx, chunk)),
        ],
        axis=1,
    )
    rows = exchange(payload)
    query_grid = rows[:, :chunk]
    key_grid = rows[:, chunk : 2 * chunk]
    halves = rows[:, 2 * chunk : 2 * chunk + 2 * own_len]
    entropy_grid = entropy_from_rows(rows[:, 2 * chunk + 2 * own_len :], chunk)
    halves = lax.all_gather(
        halves.reshape(ctx, 2, own_len, DH), "head", axis=2, tiled=True
    )
    block_keys, block_values = halves[:, 0], halves[:, 1]

    weights, left_rounded = left_step(query_grid, key_grid, entropy_grid)
    column_mass = jnp.transpose(jnp.sum(weights, axis=1), (1, 0))
    mixed = jnp.einsum(
        "pal,apd->lpd", left_rounded, query_grid, preferred_element_type=jnp.float32
    )
    query_mix = (mixed / jnp.maximum(column_mass, 1.0)[..., None]).astype(jnp.bfloat16)

    logits = jnp.einsum(
        "lpd,lid->lpi", query_mix, block_keys, preferred_element_type=jnp.float32
    ) / math.sqrt(DH)
    weights, entropy = softmax_terms(logits)
    rounded = weights.astype(jnp.bfloat16)
    key_mix = jnp.einsum(
        "lpi,lid->lpd", rounded, block_keys, preferred_element_type=jnp.float32
    ).astype(jnp.bfloat16)
    value_mix = jnp.einsum(
        "lpi,lid->lpd", rounded, block_values, preferred_element_type=jnp.float32
    ).astype(jnp.bfloat16)

    _, final_left = left_step(query_grid, key_mix, entropy)
    attended = jnp.einsum(
        "pal,lpd->apd", final_left, value_mix, preferred_element_type=jnp.float32
    ).astype(jnp.bfloat16)
    return from_dest(exchange(attended), place_count, heads_kv)


def make_local(ctx):
    def local(queries, key_states, value_states):
        keys = lax.all_gather(key_states, "head", axis=1, tiled=True)
        return jnp.stack(
            [
                one_sequence(queries[s], keys[s], key_states[s], value_states[s], ctx)
                for s in range(queries.shape[0])
            ]
        )

    return local


def solution(mesh):
    placed = P("grp", ("ctx", "head"), None)
    return jax.shard_map(
        make_local(mesh.shape["ctx"]),
        mesh=mesh,
        in_specs=(placed, placed, placed),
        out_specs=placed,
        check_vma=False,
    )
```

```python
import math

import jax
import jax.numpy as jnp
from jax import lax
from jax.sharding import PartitionSpec as P

DH = 128


def softmax_terms(logits):
    weights = jax.nn.softmax(logits, axis=-1)
    entropy = jax.nn.logsumexp(logits, axis=-1) - jnp.sum(weights * logits, axis=-1)
    return weights, entropy


def entropy_rows(flat):
    ctx, chunk = flat.shape
    high = lax.optimization_barrier(flat.astype(jnp.bfloat16))
    rest = flat - high.astype(jnp.float32)
    middle = lax.optimization_barrier(rest.astype(jnp.bfloat16))
    low = (rest - middle.astype(jnp.float32)).astype(jnp.bfloat16)
    terms = jnp.concatenate([high, middle, low], axis=1)
    row_count = -(-3 * chunk // DH)
    terms = jnp.pad(terms, ((0, 0), (0, row_count * DH - 3 * chunk)))
    return terms.reshape(ctx, row_count, DH)


def entropy_from_rows(rows, chunk):
    ctx = rows.shape[0]
    terms = rows.reshape(ctx, -1)[:, : 3 * chunk].astype(jnp.float32)
    return (terms[:, :chunk] + terms[:, chunk : 2 * chunk]) + terms[:, 2 * chunk :]


def exchange(grid):
    return lax.all_to_all(grid, "ctx", split_axis=0, concat_axis=0, tiled=True)


def left_step(query_grid, key_grid, entropy_grid):
    logits = jnp.einsum(
        "apd,lpd->pal", query_grid, key_grid, preferred_element_type=jnp.float32
    ) / math.sqrt(DH)
    logits = logits + jnp.transpose(entropy_grid, (1, 0))[:, None, :]
    weights = jax.nn.softmax(logits, axis=-1)
    return weights, weights.astype(jnp.bfloat16)


def to_dest(rows, ctx, heads_kv):
    place_count, group = rows.shape[0], rows.shape[2]
    repeat = ctx // heads_kv
    shaped = rows.reshape((repeat, place_count // repeat) + rows.shape[1:])
    shaped = jnp.moveaxis(shaped, (2, 0, 3), (0, 1, 2))
    return shaped.reshape((ctx, place_count // repeat * group) + rows.shape[3:])


def from_dest(grid, place_count, heads_kv):
    ctx = grid.shape[0]
    repeat = ctx // heads_kv
    shaped = grid.reshape(heads_kv, repeat, -1, place_count // repeat, DH)
    shaped = jnp.moveaxis(shaped, (0, 1, 2), (2, 0, 3))
    return shaped.reshape(place_count, -1)


def one_sequence(queries, keys, own_keys, own_values, ctx):
    place_count, feature_width = queries.shape
    block_len = keys.shape[0]
    heads_kv = keys.shape[1] // DH
    repeat = ctx // heads_kv
    query_heads = queries.reshape(place_count, heads_kv, -1, DH)
    key_heads = keys.reshape(block_len, heads_kv, DH)

    query_rows = to_dest(query_heads, ctx, heads_kv)
    chunk = query_rows.shape[1]
    by_head = query_rows.reshape(heads_kv, -1, DH)
    logits = jnp.einsum(
        "jpd,ijd->jpi", by_head, key_heads, preferred_element_type=jnp.float32
    ) / math.sqrt(DH)
    weights, entropy = softmax_terms(logits)
    rounded = weights.astype(jnp.bfloat16)
    key_mix = jnp.einsum(
        "jpi,ijd->jpd", rounded, key_heads, preferred_element_type=jnp.float32
    ).astype(jnp.bfloat16)

    own_len = own_keys.shape[0]
    key_rows = jnp.repeat(
        jnp.swapaxes(own_keys.reshape(own_len, heads_kv, DH), 0, 1), repeat, axis=0
    )
    value_rows = jnp.repeat(
        jnp.swapaxes(own_values.reshape(own_len, heads_kv, DH), 0, 1), repeat, axis=0
    )
    payload = jnp.concatenate(
        [
            query_rows,
            key_mix.reshape(ctx, chunk, DH),
            key_rows,
            value_rows,
            entropy_rows(entropy.reshape(ctx, chunk)),
        ],
        axis=1,
    )
    rows = exchange(payload)
    query_grid = rows[:, :chunk]
    key_grid = rows[:, chunk : 2 * chunk]
    halves = rows[:, 2 * chunk : 2 * chunk + 2 * own_len]
    entropy_grid = entropy_from_rows(rows[:, 2 * chunk + 2 * own_len :], chunk)
    mine = halves.reshape(ctx, 2, own_len, DH)
    other = lax.ppermute(mine, "head", [(0, 1), (1, 0)])
    first = lax.axis_index("head") == 0
    halves = jnp.concatenate(
        [jnp.where(first, mine, other), jnp.where(first, other, mine)], axis=2
    )
    block_keys, block_values = halves[:, 0], halves[:, 1]

    weights, left_rounded = left_step(query_grid, key_grid, entropy_grid)
    column_mass = jnp.transpose(jnp.sum(weights, axis=1), (1, 0))
    mixed = jnp.einsum(
        "pal,apd->lpd", left_rounded, query_grid, preferred_element_type=jnp.float32
    )
    query_mix = (mixed / jnp.maximum(column_mass, 1.0)[..., None]).astype(jnp.bfloat16)

    logits = jnp.einsum(
        "lpd,lid->lpi", query_mix, block_keys, preferred_element_type=jnp.float32
    ) / math.sqrt(DH)
    weights, entropy = softmax_terms(logits)
    rounded = weights.astype(jnp.bfloat16)
    key_mix = jnp.einsum(
        "lpi,lid->lpd", rounded, block_keys, preferred_element_type=jnp.float32
    ).astype(jnp.bfloat16)
    value_mix = jnp.einsum(
        "lpi,lid->lpd", rounded, block_values, preferred_element_type=jnp.float32
    ).astype(jnp.bfloat16)

    _, final_left = left_step(query_grid, key_mix, entropy)
    attended = jnp.einsum(
        "pal,lpd->apd", final_left, value_mix, preferred_element_type=jnp.float32
    ).astype(jnp.bfloat16)
    return from_dest(exchange(attended), place_count, heads_kv)


def make_local(ctx):
    def local(queries, key_states, value_states):
        keys = lax.all_gather(key_states, "head", axis=1, tiled=True)
        return jnp.stack(
            [
                one_sequence(queries[s], keys[s], key_states[s], value_states[s], ctx)
                for s in range(queries.shape[0])
            ]
        )

    return local


def solution(mesh):
    placed = P("grp", ("ctx", "head"), None)
    return jax.shard_map(
        make_local(mesh.shape["ctx"]),
        mesh=mesh,
        in_specs=(placed, placed, placed),
        out_specs=placed,
        check_vma=False,
    )
```

```python
import math

import jax
import jax.numpy as jnp
from jax import lax
from jax.sharding import PartitionSpec as P

DH = 128


def softmax_terms(logits):
    weights = jax.nn.softmax(logits, axis=-1)
    entropy = jax.nn.logsumexp(logits, axis=-1) - jnp.sum(weights * logits, axis=-1)
    return weights, entropy


def entropy_rows(flat):
    ctx, chunk = flat.shape
    high = lax.optimization_barrier(flat.astype(jnp.bfloat16))
    rest = flat - high.astype(jnp.float32)
    middle = lax.optimization_barrier(rest.astype(jnp.bfloat16))
    low = (rest - middle.astype(jnp.float32)).astype(jnp.bfloat16)
    terms = jnp.concatenate([high, middle, low], axis=1)
    row_count = -(-3 * chunk // DH)
    terms = jnp.pad(terms, ((0, 0), (0, row_count * DH - 3 * chunk)))
    return terms.reshape(ctx, row_count, DH)


def entropy_from_rows(rows, chunk):
    ctx = rows.shape[0]
    terms = rows.reshape(ctx, -1)[:, : 3 * chunk].astype(jnp.float32)
    return (terms[:, :chunk] + terms[:, chunk : 2 * chunk]) + terms[:, 2 * chunk :]


def exchange(grid):
    return lax.all_to_all(grid, "ctx", split_axis=0, concat_axis=0, tiled=True)


def left_step(query_grid, key_grid, entropy_grid):
    logits = jnp.einsum(
        "apd,lpd->pal", query_grid, key_grid, preferred_element_type=jnp.float32
    ) / math.sqrt(DH)
    logits = logits + jnp.transpose(entropy_grid, (1, 0))[:, None, :]
    weights = jax.nn.softmax(logits, axis=-1)
    return weights, weights.astype(jnp.bfloat16)


def to_dest(rows, ctx, heads_kv):
    place_count, group = rows.shape[0], rows.shape[2]
    repeat = ctx // heads_kv
    shaped = rows.reshape((repeat, place_count // repeat) + rows.shape[1:])
    shaped = jnp.moveaxis(shaped, 2, 0)
    return shaped.reshape((ctx, place_count // repeat * group) + rows.shape[3:])


def from_dest(grid, place_count, heads_kv):
    ctx = grid.shape[0]
    repeat = ctx // heads_kv
    shaped = grid.reshape(heads_kv, repeat, place_count // repeat, -1, DH)
    shaped = jnp.moveaxis(shaped, 0, 2)
    return shaped.reshape(place_count, -1)


def one_sequence(queries, keys, own_keys, own_values, ctx):
    place_count, feature_width = queries.shape
    block_len = keys.shape[0]
    heads_kv = keys.shape[1] // DH
    repeat = ctx // heads_kv
    query_heads = queries.reshape(place_count, heads_kv, -1, DH)
    key_heads = keys.reshape(block_len, heads_kv, DH)

    query_rows = to_dest(query_heads, ctx, heads_kv)
    chunk = query_rows.shape[1]
    by_head = query_rows.reshape(heads_kv, -1, DH)
    logits = jnp.einsum(
        "jpd,ijd->jpi", by_head, key_heads, preferred_element_type=jnp.float32
    ) / math.sqrt(DH)
    weights, entropy = softmax_terms(logits)
    rounded = weights.astype(jnp.bfloat16)
    key_mix = jnp.einsum(
        "jpi,ijd->jpd", rounded, key_heads, preferred_element_type=jnp.float32
    ).astype(jnp.bfloat16)

    own_len = own_keys.shape[0]
    key_rows = jnp.repeat(
        jnp.swapaxes(own_keys.reshape(own_len, heads_kv, DH), 0, 1), repeat, axis=0
    )
    value_rows = jnp.repeat(
        jnp.swapaxes(own_values.reshape(own_len, heads_kv, DH), 0, 1), repeat, axis=0
    )
    payload = jnp.concatenate(
        [
            query_rows,
            key_mix.reshape(ctx, chunk, DH),
            key_rows,
            value_rows,
            entropy_rows(entropy.reshape(ctx, chunk)),
        ],
        axis=1,
    )
    rows = exchange(payload)
    query_grid = rows[:, :chunk]
    key_grid = rows[:, chunk : 2 * chunk]
    halves = rows[:, 2 * chunk : 2 * chunk + 2 * own_len]
    entropy_grid = entropy_from_rows(rows[:, 2 * chunk + 2 * own_len :], chunk)
    mine = halves.reshape(ctx, 2, own_len, DH)
    other = lax.ppermute(mine, "head", [(0, 1), (1, 0)])
    first = lax.axis_index("head") == 0
    halves = jnp.concatenate(
        [jnp.where(first, mine, other), jnp.where(first, other, mine)], axis=2
    )
    block_keys, block_values = halves[:, 0], halves[:, 1]

    weights, left_rounded = left_step(query_grid, key_grid, entropy_grid)
    column_mass = jnp.transpose(jnp.sum(weights, axis=1), (1, 0))
    mixed = jnp.einsum(
        "pal,apd->lpd", left_rounded, query_grid, preferred_element_type=jnp.float32
    )
    query_mix = (mixed / jnp.maximum(column_mass, 1.0)[..., None]).astype(jnp.bfloat16)

    logits = jnp.einsum(
        "lpd,lid->lpi", query_mix, block_keys, preferred_element_type=jnp.float32
    ) / math.sqrt(DH)
    weights, entropy = softmax_terms(logits)
    rounded = weights.astype(jnp.bfloat16)
    key_mix = jnp.einsum(
        "lpi,lid->lpd", rounded, block_keys, preferred_element_type=jnp.float32
    ).astype(jnp.bfloat16)
    value_mix = jnp.einsum(
        "lpi,lid->lpd", rounded, block_values, preferred_element_type=jnp.float32
    ).astype(jnp.bfloat16)

    _, final_left = left_step(query_grid, key_mix, entropy)
    attended = jnp.einsum(
        "pal,lpd->apd", final_left, value_mix, preferred_element_type=jnp.float32
    ).astype(jnp.bfloat16)
    return from_dest(exchange(attended), place_count, heads_kv)


def make_local(ctx):
    def local(queries, key_states, value_states):
        keys = lax.all_gather(key_states, "head", axis=1, tiled=True)
        return jnp.stack(
            [
                one_sequence(queries[s], keys[s], key_states[s], value_states[s], ctx)
                for s in range(queries.shape[0])
            ]
        )

    return local


def solution(mesh):
    placed = P("grp", ("ctx", "head"), None)
    return jax.shard_map(
        make_local(mesh.shape["ctx"]),
        mesh=mesh,
        in_specs=(placed, placed, placed),
        out_specs=placed,
        check_vma=False,
    )
```

```python
import math

import jax
import jax.numpy as jnp
from jax import lax
from jax.sharding import PartitionSpec as P

DH = 128


def softmax_terms(logits):
    weights = jax.nn.softmax(logits, axis=-1)
    entropy = jax.nn.logsumexp(logits, axis=-1) - jnp.sum(weights * logits, axis=-1)
    return weights, entropy


def exchange(grid):
    return lax.all_to_all(grid, "ctx", split_axis=0, concat_axis=0, tiled=True)


def left_step(query_grid, key_grid, entropy_grid):
    logits = jnp.einsum(
        "apd,lpd->pal", query_grid, key_grid, preferred_element_type=jnp.float32
    ) / math.sqrt(DH)
    logits = logits + jnp.transpose(entropy_grid, (1, 0))[:, None, :]
    weights = jax.nn.softmax(logits, axis=-1)
    return weights, weights.astype(jnp.bfloat16)


def to_dest(rows, ctx, heads_kv):
    place_count, group = rows.shape[0], rows.shape[2]
    repeat = ctx // heads_kv
    shaped = rows.reshape((repeat, place_count // repeat) + rows.shape[1:])
    shaped = jnp.moveaxis(shaped, 2, 0)
    return shaped.reshape((ctx, place_count // repeat * group) + rows.shape[3:])


def from_dest(grid, place_count, heads_kv):
    ctx = grid.shape[0]
    repeat = ctx // heads_kv
    shaped = grid.reshape(heads_kv, repeat, place_count // repeat, -1, DH)
    shaped = jnp.moveaxis(shaped, 0, 2)
    return shaped.reshape(place_count, -1)


def right_step(query_grid, block_keys):
    logits = jnp.einsum(
        "lpd,lid->lpi", query_grid, block_keys, preferred_element_type=jnp.float32
    ) / math.sqrt(DH)
    weights, entropy = softmax_terms(logits)
    rounded = weights.astype(jnp.bfloat16)
    key_mix = jnp.einsum(
        "lpi,lid->lpd", rounded, block_keys, preferred_element_type=jnp.float32
    ).astype(jnp.bfloat16)
    return rounded, entropy, key_mix


def one_sequence(queries, own_keys, own_values, ctx):
    place_count, feature_width = queries.shape
    own_len = own_keys.shape[0]
    heads_kv = own_keys.shape[1] // DH
    repeat = ctx // heads_kv
    query_rows = to_dest(queries.reshape(place_count, heads_kv, -1, DH), ctx, heads_kv)
    chunk = query_rows.shape[1]
    key_rows = jnp.repeat(
        jnp.swapaxes(own_keys.reshape(own_len, heads_kv, DH), 0, 1), repeat, axis=0
    )
    value_rows = jnp.repeat(
        jnp.swapaxes(own_values.reshape(own_len, heads_kv, DH), 0, 1), repeat, axis=0
    )
    rows = exchange(jnp.concatenate([query_rows, key_rows, value_rows], axis=1))
    query_grid = rows[:, :chunk]
    halves = lax.all_gather(
        rows[:, chunk:].reshape(ctx, 2, own_len, DH), "head", axis=2, tiled=True
    )
    block_keys, block_values = halves[:, 0], halves[:, 1]

    _, entropy_grid, key_grid = right_step(query_grid, block_keys)
    weights, left_rounded = left_step(query_grid, key_grid, entropy_grid)
    column_mass = jnp.transpose(jnp.sum(weights, axis=1), (1, 0))
    mixed = jnp.einsum(
        "pal,apd->lpd", left_rounded, query_grid, preferred_element_type=jnp.float32
    )
    query_mix = (mixed / jnp.maximum(column_mass, 1.0)[..., None]).astype(jnp.bfloat16)

    rounded, entropy, key_mix = right_step(query_mix, block_keys)
    value_mix = jnp.einsum(
        "lpi,lid->lpd", rounded, block_values, preferred_element_type=jnp.float32
    ).astype(jnp.bfloat16)

    _, final_left = left_step(query_grid, key_mix, entropy)
    attended = jnp.einsum(
        "pal,lpd->apd", final_left, value_mix, preferred_element_type=jnp.float32
    ).astype(jnp.bfloat16)
    return from_dest(exchange(attended), place_count, heads_kv)


def make_local(ctx):
    def local(queries, key_states, value_states):
        return jnp.stack(
            [
                one_sequence(queries[s], key_states[s], value_states[s], ctx)
                for s in range(queries.shape[0])
            ]
        )

    return local


def solution(mesh):
    placed = P("grp", ("ctx", "head"), None)
    return jax.shard_map(
        make_local(mesh.shape["ctx"]),
        mesh=mesh,
        in_specs=(placed, placed, placed),
        out_specs=placed,
        check_vma=False,
    )
```

```python
import math

import jax
import jax.numpy as jnp
from jax import lax
from jax.experimental import pallas as pl
from jax.sharding import PartitionSpec as P

DH = 128


def softmax_terms(logits):
    weights = jax.nn.softmax(logits, axis=-1)
    entropy = jax.nn.logsumexp(logits, axis=-1) - jnp.sum(weights * logits, axis=-1)
    return weights, entropy


def exchange(grid):
    return lax.all_to_all(grid, "ctx", split_axis=0, concat_axis=0, tiled=True)


def left_step(query_grid, key_grid, entropy_grid):
    logits = jnp.einsum(
        "apd,lpd->pal", query_grid, key_grid, preferred_element_type=jnp.float32
    ) / math.sqrt(DH)
    logits = logits + jnp.transpose(entropy_grid, (1, 0))[:, None, :]
    weights = jax.nn.softmax(logits, axis=-1)
    return weights, weights.astype(jnp.bfloat16)


def to_dest(rows, ctx, heads_kv):
    place_count, group = rows.shape[0], rows.shape[2]
    repeat = ctx // heads_kv
    shaped = rows.reshape((repeat, place_count // repeat) + rows.shape[1:])
    shaped = jnp.moveaxis(shaped, (2, 0, 3), (0, 1, 2))
    return shaped.reshape((ctx, place_count // repeat * group) + rows.shape[3:])


def from_dest(grid, place_count, heads_kv):
    ctx = grid.shape[0]
    repeat = ctx // heads_kv
    shaped = grid.reshape(heads_kv, repeat, -1, place_count // repeat, DH)
    shaped = jnp.moveaxis(shaped, (0, 1, 2), (2, 0, 3))
    return shaped.reshape(place_count, -1)


def pack_kernel(query_ref, key_ref, value_ref, out_ref):
    place_count = query_ref.shape[0]
    ctx = out_ref.shape[0]
    group = query_ref.shape[1] // key_ref.shape[1]
    for dest in range(ctx):
        for g in range(group):
            head = dest * group + g
            out_ref[dest, g * place_count : (g + 1) * place_count, :] = query_ref[
                :, head * DH : (head + 1) * DH
            ]
        base = group * place_count
        out_ref[dest, base : base + place_count, :] = key_ref[:, dest * DH : (dest + 1) * DH]
        base += place_count
        out_ref[dest, base : base + place_count, :] = value_ref[:, dest * DH : (dest + 1) * DH]


def unpack_kernel(grid_ref, out_ref):
    ctx, rows, _ = grid_ref.shape
    place_count = out_ref.shape[0]
    group = rows // place_count
    for source in range(ctx):
        for g in range(group):
            head = source * group + g
            out_ref[:, head * DH : (head + 1) * DH] = grid_ref[
                source, g * place_count : (g + 1) * place_count, :
            ]


def pack(queries, own_keys, own_values, ctx):
    place_count = queries.shape[0]
    heads_kv = own_keys.shape[1] // DH
    if ctx != heads_kv:
        repeat = ctx // heads_kv
        query_rows = to_dest(queries.reshape(place_count, heads_kv, -1, DH), ctx, heads_kv)
        key_rows = jnp.repeat(
            jnp.swapaxes(own_keys.reshape(place_count, heads_kv, DH), 0, 1), repeat, axis=0
        )
        value_rows = jnp.repeat(
            jnp.swapaxes(own_values.reshape(place_count, heads_kv, DH), 0, 1), repeat, axis=0
        )
        return jnp.concatenate([query_rows, key_rows, value_rows], axis=1)
    rows = queries.shape[1] // DH // heads_kv * place_count + 2 * place_count
    return pl.pallas_call(
        pack_kernel, out_shape=jax.ShapeDtypeStruct((ctx, rows, DH), queries.dtype)
    )(queries, own_keys, own_values)


def unpack(grid, place_count, heads_kv):
    ctx, rows, _ = grid.shape
    if ctx != heads_kv:
        return from_dest(grid, place_count, heads_kv)
    return pl.pallas_call(
        unpack_kernel,
        out_shape=jax.ShapeDtypeStruct((place_count, ctx * rows // place_count * DH), grid.dtype),
    )(grid)


def right_step(query_grid, block_keys):
    logits = jnp.einsum(
        "lpd,lid->lpi", query_grid, block_keys, preferred_element_type=jnp.float32
    ) / math.sqrt(DH)
    weights, entropy = softmax_terms(logits)
    rounded = weights.astype(jnp.bfloat16)
    key_mix = jnp.einsum(
        "lpi,lid->lpd", rounded, block_keys, preferred_element_type=jnp.float32
    ).astype(jnp.bfloat16)
    return rounded, entropy, key_mix


def one_sequence(queries, own_keys, own_values, ctx):
    place_count, feature_width = queries.shape
    own_len = own_keys.shape[0]
    heads_kv = own_keys.shape[1] // DH
    chunk = feature_width // DH * place_count // ctx
    rows = exchange(pack(queries, own_keys, own_values, ctx))
    query_grid = rows[:, :chunk]
    halves = lax.all_gather(
        rows[:, chunk:].reshape(ctx, 2, own_len, DH), "head", axis=2, tiled=True
    )
    block_keys, block_values = halves[:, 0], halves[:, 1]

    _, entropy_grid, key_grid = right_step(query_grid, block_keys)
    weights, left_rounded = left_step(query_grid, key_grid, entropy_grid)
    column_mass = jnp.transpose(jnp.sum(weights, axis=1), (1, 0))
    mixed = jnp.einsum(
        "pal,apd->lpd", left_rounded, query_grid, preferred_element_type=jnp.float32
    )
    query_mix = (mixed / jnp.maximum(column_mass, 1.0)[..., None]).astype(jnp.bfloat16)

    rounded, entropy, key_mix = right_step(query_mix, block_keys)
    value_mix = jnp.einsum(
        "lpi,lid->lpd", rounded, block_values, preferred_element_type=jnp.float32
    ).astype(jnp.bfloat16)

    _, final_left = left_step(query_grid, key_mix, entropy)
    attended = jnp.einsum(
        "pal,lpd->apd", final_left, value_mix, preferred_element_type=jnp.float32
    ).astype(jnp.bfloat16)
    return unpack(exchange(attended), place_count, heads_kv)


def make_local(ctx):
    def local(queries, key_states, value_states):
        return jnp.stack(
            [
                one_sequence(queries[s], key_states[s], value_states[s], ctx)
                for s in range(queries.shape[0])
            ]
        )

    return local


def solution(mesh):
    placed = P("grp", ("ctx", "head"), None)
    return jax.shard_map(
        make_local(mesh.shape["ctx"]),
        mesh=mesh,
        in_specs=(placed, placed, placed),
        out_specs=placed,
        check_vma=False,
    )
```

```python
import math

import jax
import jax.numpy as jnp
from jax import lax
from jax.experimental import pallas as pl
from jax.sharding import PartitionSpec as P

DH = 128


def softmax_terms(logits):
    weights = jax.nn.softmax(logits, axis=-1)
    entropy = jax.nn.logsumexp(logits, axis=-1) - jnp.sum(weights * logits, axis=-1)
    return weights, entropy


def exchange(grid):
    return lax.all_to_all(grid, "ctx", split_axis=0, concat_axis=0, tiled=True)


def left_step(query_grid, key_grid, entropy_grid):
    logits = jnp.einsum(
        "apd,lpd->pal", query_grid, key_grid, preferred_element_type=jnp.float32
    ) / math.sqrt(DH)
    logits = logits + jnp.transpose(entropy_grid, (1, 0))[:, None, :]
    weights = jax.nn.softmax(logits, axis=-1)
    return weights, weights.astype(jnp.bfloat16)


def to_dest(rows, ctx, heads_kv):
    place_count, group = rows.shape[0], rows.shape[2]
    repeat = ctx // heads_kv
    shaped = rows.reshape((repeat, place_count // repeat) + rows.shape[1:])
    shaped = jnp.moveaxis(shaped, (2, 0, 3), (0, 1, 2))
    return shaped.reshape((ctx, place_count // repeat * group) + rows.shape[3:])


def from_dest(grid, place_count, heads_kv):
    ctx = grid.shape[0]
    repeat = ctx // heads_kv
    shaped = grid.reshape(heads_kv, repeat, -1, place_count // repeat, DH)
    shaped = jnp.moveaxis(shaped, (0, 1, 2), (2, 0, 3))
    return shaped.reshape(place_count, -1)


def pack_kernel(query_ref, key_ref, value_ref, out_ref):
    place_count = query_ref.shape[0]
    ctx = out_ref.shape[0]
    group = query_ref.shape[1] // key_ref.shape[1]
    for dest in range(ctx):
        for g in range(group):
            head = dest * group + g
            out_ref[dest, g * place_count : (g + 1) * place_count, :] = query_ref[
                :, head * DH : (head + 1) * DH
            ]
        base = group * place_count
        out_ref[dest, base : base + place_count, :] = key_ref[:, dest * DH : (dest + 1) * DH]
        base += place_count
        out_ref[dest, base : base + place_count, :] = value_ref[:, dest * DH : (dest + 1) * DH]


def pack(queries, own_keys, own_values, ctx):
    place_count = queries.shape[0]
    heads_kv = own_keys.shape[1] // DH
    if ctx != heads_kv:
        repeat = ctx // heads_kv
        query_rows = to_dest(queries.reshape(place_count, heads_kv, -1, DH), ctx, heads_kv)
        key_rows = jnp.repeat(
            jnp.swapaxes(own_keys.reshape(place_count, heads_kv, DH), 0, 1), repeat, axis=0
        )
        value_rows = jnp.repeat(
            jnp.swapaxes(own_values.reshape(place_count, heads_kv, DH), 0, 1), repeat, axis=0
        )
        return jnp.concatenate([query_rows, key_rows, value_rows], axis=1)
    rows = queries.shape[1] // DH // heads_kv * place_count + 2 * place_count
    return pl.pallas_call(
        pack_kernel, out_shape=jax.ShapeDtypeStruct((ctx, rows, DH), queries.dtype)
    )(queries, own_keys, own_values)


def right_step(query_grid, block_keys):
    logits = jnp.einsum(
        "lpd,lid->lpi", query_grid, block_keys, preferred_element_type=jnp.float32
    ) / math.sqrt(DH)
    weights, entropy = softmax_terms(logits)
    rounded = weights.astype(jnp.bfloat16)
    key_mix = jnp.einsum(
        "lpi,lid->lpd", rounded, block_keys, preferred_element_type=jnp.float32
    ).astype(jnp.bfloat16)
    return rounded, entropy, key_mix


def one_sequence(queries, own_keys, own_values, ctx):
    place_count, feature_width = queries.shape
    own_len = own_keys.shape[0]
    heads_kv = own_keys.shape[1] // DH
    chunk = feature_width // DH * place_count // ctx
    rows = exchange(pack(queries, own_keys, own_values, ctx))
    query_grid = rows[:, :chunk]
    halves = lax.all_gather(
        rows[:, chunk:].reshape(ctx, 2, own_len, DH), "head", axis=2, tiled=True
    )
    block_keys, block_values = halves[:, 0], halves[:, 1]

    _, entropy_grid, key_grid = right_step(query_grid, block_keys)
    weights, left_rounded = left_step(query_grid, key_grid, entropy_grid)
    column_mass = jnp.transpose(jnp.sum(weights, axis=1), (1, 0))
    mixed = jnp.einsum(
        "pal,apd->lpd", left_rounded, query_grid, preferred_element_type=jnp.float32
    )
    query_mix = (mixed / jnp.maximum(column_mass, 1.0)[..., None]).astype(jnp.bfloat16)

    rounded, entropy, key_mix = right_step(query_mix, block_keys)
    value_mix = jnp.einsum(
        "lpi,lid->lpd", rounded, block_values, preferred_element_type=jnp.float32
    ).astype(jnp.bfloat16)

    _, final_left = left_step(query_grid, key_mix, entropy)
    attended = jnp.einsum(
        "pal,lpd->apd", final_left, value_mix, preferred_element_type=jnp.float32
    ).astype(jnp.bfloat16)
    return from_dest(exchange(attended), place_count, heads_kv)


def make_local(ctx):
    def local(queries, key_states, value_states):
        return jnp.stack(
            [
                one_sequence(queries[s], key_states[s], value_states[s], ctx)
                for s in range(queries.shape[0])
            ]
        )

    return local


def solution(mesh):
    placed = P("grp", ("ctx", "head"), None)
    return jax.shard_map(
        make_local(mesh.shape["ctx"]),
        mesh=mesh,
        in_specs=(placed, placed, placed),
        out_specs=placed,
        check_vma=False,
    )
```

```python
import math

import jax
import jax.numpy as jnp
from jax import lax
from jax.experimental import pallas as pl
from jax.sharding import PartitionSpec as P

DH = 128


def softmax_terms(logits):
    weights = jax.nn.softmax(logits, axis=-1)
    entropy = jax.nn.logsumexp(logits, axis=-1) - jnp.sum(weights * logits, axis=-1)
    return weights, entropy


def exchange(grid):
    return lax.all_to_all(grid, "ctx", split_axis=0, concat_axis=0, tiled=True)


def pair_logits(query_grid, key_grid):
    blocks, pairs, _ = query_grid.shape
    tile = 16 if pairs % 16 == 0 else pairs
    groups = pairs // tile

    def grouped(grid):
        shaped = grid.reshape(blocks, groups, tile, DH)
        return jnp.transpose(shaped, (1, 2, 0, 3)).reshape(groups, tile * blocks, DH)

    products = jnp.einsum(
        "gxd,gyd->gxy", grouped(query_grid), grouped(key_grid),
        preferred_element_type=jnp.float32,
    )
    index = jnp.arange(tile * blocks)
    same_pair = (index[:, None] // blocks) == (index[None, :] // blocks)
    select = (index[:, None] % blocks == jnp.arange(blocks)[None, :]).astype(jnp.float32)
    folded = jnp.einsum(
        "gxy,yl->gxl", jnp.where(same_pair, products, 0.0), select,
        precision=lax.Precision.HIGHEST,
    )
    return folded.reshape(pairs, blocks, blocks)


def left_step(query_grid, key_grid, entropy_grid):
    logits = pair_logits(query_grid, key_grid) / math.sqrt(DH)
    logits = logits + jnp.transpose(entropy_grid, (1, 0))[:, None, :]
    weights = jax.nn.softmax(logits, axis=-1)
    return weights, weights.astype(jnp.bfloat16)


def to_dest(rows, ctx, heads_kv):
    place_count, group = rows.shape[0], rows.shape[2]
    repeat = ctx // heads_kv
    shaped = rows.reshape((repeat, place_count // repeat) + rows.shape[1:])
    shaped = jnp.moveaxis(shaped, (2, 0, 3), (0, 1, 2))
    return shaped.reshape((ctx, place_count // repeat * group) + rows.shape[3:])


def from_dest(grid, place_count, heads_kv):
    ctx = grid.shape[0]
    repeat = ctx // heads_kv
    shaped = grid.reshape(heads_kv, repeat, -1, place_count // repeat, DH)
    shaped = jnp.moveaxis(shaped, (0, 1, 2), (2, 0, 3))
    return shaped.reshape(place_count, -1)


def pack_kernel(query_ref, key_ref, value_ref, out_ref):
    place_count = query_ref.shape[0]
    ctx = out_ref.shape[0]
    group = query_ref.shape[1] // key_ref.shape[1]
    for dest in range(ctx):
        for g in range(group):
            head = dest * group + g
            out_ref[dest, g * place_count : (g + 1) * place_count, :] = query_ref[
                :, head * DH : (head + 1) * DH
            ]
        base = group * place_count
        out_ref[dest, base : base + place_count, :] = key_ref[:, dest * DH : (dest + 1) * DH]
        base += place_count
        out_ref[dest, base : base + place_count, :] = value_ref[:, dest * DH : (dest + 1) * DH]


def pack(queries, own_keys, own_values, ctx):
    place_count = queries.shape[0]
    heads_kv = own_keys.shape[1] // DH
    if ctx != heads_kv:
        repeat = ctx // heads_kv
        query_rows = to_dest(queries.reshape(place_count, heads_kv, -1, DH), ctx, heads_kv)
        key_rows = jnp.repeat(
            jnp.swapaxes(own_keys.reshape(place_count, heads_kv, DH), 0, 1), repeat, axis=0
        )
        value_rows = jnp.repeat(
            jnp.swapaxes(own_values.reshape(place_count, heads_kv, DH), 0, 1), repeat, axis=0
        )
        return jnp.concatenate([query_rows, key_rows, value_rows], axis=1)
    rows = queries.shape[1] // DH // heads_kv * place_count + 2 * place_count
    return pl.pallas_call(
        pack_kernel, out_shape=jax.ShapeDtypeStruct((ctx, rows, DH), queries.dtype)
    )(queries, own_keys, own_values)


def right_step(query_grid, block_keys):
    logits = jnp.einsum(
        "lpd,lid->lpi", query_grid, block_keys, preferred_element_type=jnp.float32
    ) / math.sqrt(DH)
    weights, entropy = softmax_terms(logits)
    rounded = weights.astype(jnp.bfloat16)
    key_mix = jnp.einsum(
        "lpi,lid->lpd", rounded, block_keys, preferred_element_type=jnp.float32
    ).astype(jnp.bfloat16)
    return rounded, entropy, key_mix


def one_sequence(queries, own_keys, own_values, ctx):
    place_count, feature_width = queries.shape
    own_len = own_keys.shape[0]
    heads_kv = own_keys.shape[1] // DH
    chunk = feature_width // DH * place_count // ctx
    rows = exchange(pack(queries, own_keys, own_values, ctx))
    query_grid = rows[:, :chunk]
    halves = lax.all_gather(
        rows[:, chunk:].reshape(ctx, 2, own_len, DH), "head", axis=2, tiled=True
    )
    block_keys, block_values = halves[:, 0], halves[:, 1]

    _, entropy_grid, key_grid = right_step(query_grid, block_keys)
    weights, left_rounded = left_step(query_grid, key_grid, entropy_grid)
    column_mass = jnp.transpose(jnp.sum(weights, axis=1), (1, 0))
    mixed = jnp.einsum(
        "pal,apd->lpd", left_rounded, query_grid, preferred_element_type=jnp.float32
    )
    query_mix = (mixed / jnp.maximum(column_mass, 1.0)[..., None]).astype(jnp.bfloat16)

    rounded, entropy, key_mix = right_step(query_mix, block_keys)
    value_mix = jnp.einsum(
        "lpi,lid->lpd", rounded, block_values, preferred_element_type=jnp.float32
    ).astype(jnp.bfloat16)

    _, final_left = left_step(query_grid, key_mix, entropy)
    attended = jnp.einsum(
        "pal,lpd->apd", final_left, value_mix, preferred_element_type=jnp.float32
    ).astype(jnp.bfloat16)
    return from_dest(exchange(attended), place_count, heads_kv)


def make_local(ctx):
    def local(queries, key_states, value_states):
        return jnp.stack(
            [
                one_sequence(queries[s], key_states[s], value_states[s], ctx)
                for s in range(queries.shape[0])
            ]
        )

    return local


def solution(mesh):
    placed = P("grp", ("ctx", "head"), None)
    return jax.shard_map(
        make_local(mesh.shape["ctx"]),
        mesh=mesh,
        in_specs=(placed, placed, placed),
        out_specs=placed,
        check_vma=False,
    )
```

```python
import math

import jax
import jax.numpy as jnp
from jax import lax
from jax.experimental import pallas as pl
from jax.experimental.pallas import tpu as pltpu
from jax.sharding import PartitionSpec as P

DH = 128


def softmax_terms(logits):
    weights = jax.nn.softmax(logits, axis=-1)
    entropy = jax.nn.logsumexp(logits, axis=-1) - jnp.sum(weights * logits, axis=-1)
    return weights, entropy


def exchange(grid):
    return lax.all_to_all(grid, "ctx", split_axis=0, concat_axis=0, tiled=True)


def left_step(query_grid, key_grid, entropy_grid):
    logits = jnp.einsum(
        "apd,lpd->pal", query_grid, key_grid, preferred_element_type=jnp.float32
    ) / math.sqrt(DH)
    logits = logits + jnp.transpose(entropy_grid, (1, 0))[:, None, :]
    weights = jax.nn.softmax(logits, axis=-1)
    return weights, weights.astype(jnp.bfloat16)


def to_dest(rows, ctx, heads_kv):
    place_count, group = rows.shape[0], rows.shape[2]
    repeat = ctx // heads_kv
    shaped = rows.reshape((repeat, place_count // repeat) + rows.shape[1:])
    shaped = jnp.moveaxis(shaped, (2, 0, 3), (0, 1, 2))
    return shaped.reshape((ctx, place_count // repeat * group) + rows.shape[3:])


def from_dest(grid, place_count, heads_kv):
    ctx = grid.shape[0]
    repeat = ctx // heads_kv
    shaped = grid.reshape(heads_kv, repeat, -1, place_count // repeat, DH)
    shaped = jnp.moveaxis(shaped, (0, 1, 2), (2, 0, 3))
    return shaped.reshape(place_count, -1)


def pack_kernel(query_ref, key_ref, value_ref, out_ref, sems):
    place_count = query_ref.shape[0]
    ctx = out_ref.shape[0]
    group = query_ref.shape[1] // key_ref.shape[1]
    moves = []
    for dest in range(ctx):
        for g in range(group):
            head = dest * group + g
            moves.append(
                (query_ref.at[:, pl.ds(head * DH, DH)], out_ref.at[dest, pl.ds(g * place_count, place_count)])
            )
        base = group * place_count
        moves.append((key_ref.at[:, pl.ds(dest * DH, DH)], out_ref.at[dest, pl.ds(base, place_count)]))
        base += place_count
        moves.append((value_ref.at[:, pl.ds(dest * DH, DH)], out_ref.at[dest, pl.ds(base, place_count)]))
    copies = [
        pltpu.make_async_copy(source, target, sems.at[index])
        for index, (source, target) in enumerate(moves)
    ]
    for copy in copies:
        copy.start()
    for copy in copies:
        copy.wait()


def unpack_kernel(grid_ref, out_ref, sems):
    ctx, rows, _ = grid_ref.shape
    place_count = out_ref.shape[0]
    group = rows // place_count
    copies = []
    for source in range(ctx):
        for g in range(group):
            head = source * group + g
            copies.append(
                pltpu.make_async_copy(
                    grid_ref.at[source, pl.ds(g * place_count, place_count)],
                    out_ref.at[:, pl.ds(head * DH, DH)],
                    sems.at[len(copies)],
                )
            )
    for copy in copies:
        copy.start()
    for copy in copies:
        copy.wait()


def pack(queries, own_keys, own_values, ctx):
    place_count = queries.shape[0]
    heads_kv = own_keys.shape[1] // DH
    if ctx != heads_kv:
        repeat = ctx // heads_kv
        query_rows = to_dest(queries.reshape(place_count, heads_kv, -1, DH), ctx, heads_kv)
        key_rows = jnp.repeat(
            jnp.swapaxes(own_keys.reshape(place_count, heads_kv, DH), 0, 1), repeat, axis=0
        )
        value_rows = jnp.repeat(
            jnp.swapaxes(own_values.reshape(place_count, heads_kv, DH), 0, 1), repeat, axis=0
        )
        return jnp.concatenate([query_rows, key_rows, value_rows], axis=1)
    rows = queries.shape[1] // DH // heads_kv * place_count + 2 * place_count
    anywhere = pl.BlockSpec(memory_space=pl.ANY)
    return pl.pallas_call(
        pack_kernel,
        out_shape=jax.ShapeDtypeStruct((ctx, rows, DH), queries.dtype),
        in_specs=[anywhere, anywhere, anywhere],
        out_specs=anywhere,
        scratch_shapes=[pltpu.SemaphoreType.DMA((ctx * (queries.shape[1] // DH // heads_kv + 2),))],
    )(queries, own_keys, own_values)


def unpack(grid, place_count, heads_kv):
    ctx, rows, _ = grid.shape
    if ctx != heads_kv:
        return from_dest(grid, place_count, heads_kv)
    anywhere = pl.BlockSpec(memory_space=pl.ANY)
    heads = ctx * rows // place_count
    return pl.pallas_call(
        unpack_kernel,
        out_shape=jax.ShapeDtypeStruct((place_count, heads * DH), grid.dtype),
        in_specs=[anywhere],
        out_specs=anywhere,
        scratch_shapes=[pltpu.SemaphoreType.DMA((heads,))],
    )(grid)


def right_step(query_grid, block_keys):
    logits = jnp.einsum(
        "lpd,lid->lpi", query_grid, block_keys, preferred_element_type=jnp.float32
    ) / math.sqrt(DH)
    weights, entropy = softmax_terms(logits)
    rounded = weights.astype(jnp.bfloat16)
    key_mix = jnp.einsum(
        "lpi,lid->lpd", rounded, block_keys, preferred_element_type=jnp.float32
    ).astype(jnp.bfloat16)
    return rounded, entropy, key_mix


def one_sequence(queries, own_keys, own_values, ctx):
    place_count, feature_width = queries.shape
    own_len = own_keys.shape[0]
    heads_kv = own_keys.shape[1] // DH
    chunk = feature_width // DH * place_count // ctx
    rows = exchange(pack(queries, own_keys, own_values, ctx))
    query_grid = rows[:, :chunk]
    halves = lax.all_gather(
        rows[:, chunk:].reshape(ctx, 2, own_len, DH), "head", axis=2, tiled=True
    )
    block_keys, block_values = halves[:, 0], halves[:, 1]

    _, entropy_grid, key_grid = right_step(query_grid, block_keys)
    weights, left_rounded = left_step(query_grid, key_grid, entropy_grid)
    column_mass = jnp.transpose(jnp.sum(weights, axis=1), (1, 0))
    mixed = jnp.einsum(
        "pal,apd->lpd", left_rounded, query_grid, preferred_element_type=jnp.float32
    )
    query_mix = (mixed / jnp.maximum(column_mass, 1.0)[..., None]).astype(jnp.bfloat16)

    rounded, entropy, key_mix = right_step(query_mix, block_keys)
    value_mix = jnp.einsum(
        "lpi,lid->lpd", rounded, block_values, preferred_element_type=jnp.float32
    ).astype(jnp.bfloat16)

    _, final_left = left_step(query_grid, key_mix, entropy)
    attended = jnp.einsum(
        "pal,lpd->apd", final_left, value_mix, preferred_element_type=jnp.float32
    ).astype(jnp.bfloat16)
    return unpack(exchange(attended), place_count, heads_kv)


def make_local(ctx):
    def local(queries, key_states, value_states):
        return jnp.stack(
            [
                one_sequence(queries[s], key_states[s], value_states[s], ctx)
                for s in range(queries.shape[0])
            ]
        )

    return local


def solution(mesh):
    placed = P("grp", ("ctx", "head"), None)
    return jax.shard_map(
        make_local(mesh.shape["ctx"]),
        mesh=mesh,
        in_specs=(placed, placed, placed),
        out_specs=placed,
        check_vma=False,
    )
```

```python
import math

import jax
import jax.numpy as jnp
from jax import lax
from jax.experimental import pallas as pl
from jax.sharding import PartitionSpec as P

DH = 128


def softmax_terms(logits):
    weights = jax.nn.softmax(logits, axis=-1)
    entropy = jax.nn.logsumexp(logits, axis=-1) - jnp.sum(weights * logits, axis=-1)
    return weights, entropy


def exchange(grid):
    return lax.all_to_all(grid, "ctx", split_axis=0, concat_axis=0, tiled=True)


def left_step(query_grid, key_grid, entropy_grid):
    logits = jnp.einsum(
        "apd,lpd->alp", query_grid, key_grid, preferred_element_type=jnp.float32
    ) / math.sqrt(DH)
    logits = logits + entropy_grid[None]
    weights = jax.nn.softmax(logits, axis=1)
    return weights, weights.astype(jnp.bfloat16)


def to_dest(rows, ctx, heads_kv):
    place_count, group = rows.shape[0], rows.shape[2]
    repeat = ctx // heads_kv
    shaped = rows.reshape((repeat, place_count // repeat) + rows.shape[1:])
    shaped = jnp.moveaxis(shaped, (2, 0, 3), (0, 1, 2))
    return shaped.reshape((ctx, place_count // repeat * group) + rows.shape[3:])


def from_dest(grid, place_count, heads_kv):
    ctx = grid.shape[0]
    repeat = ctx // heads_kv
    shaped = grid.reshape(heads_kv, repeat, -1, place_count // repeat, DH)
    shaped = jnp.moveaxis(shaped, (0, 1, 2), (2, 0, 3))
    return shaped.reshape(place_count, -1)


def pack_kernel(query_ref, key_ref, value_ref, out_ref):
    place_count = query_ref.shape[0]
    ctx = out_ref.shape[0]
    group = query_ref.shape[1] // key_ref.shape[1]
    for dest in range(ctx):
        for g in range(group):
            head = dest * group + g
            out_ref[dest, g * place_count : (g + 1) * place_count, :] = query_ref[
                :, head * DH : (head + 1) * DH
            ]
        base = group * place_count
        out_ref[dest, base : base + place_count, :] = key_ref[:, dest * DH : (dest + 1) * DH]
        base += place_count
        out_ref[dest, base : base + place_count, :] = value_ref[:, dest * DH : (dest + 1) * DH]


def pack(queries, own_keys, own_values, ctx):
    place_count = queries.shape[0]
    heads_kv = own_keys.shape[1] // DH
    if ctx != heads_kv:
        repeat = ctx // heads_kv
        query_rows = to_dest(queries.reshape(place_count, heads_kv, -1, DH), ctx, heads_kv)
        key_rows = jnp.repeat(
            jnp.swapaxes(own_keys.reshape(place_count, heads_kv, DH), 0, 1), repeat, axis=0
        )
        value_rows = jnp.repeat(
            jnp.swapaxes(own_values.reshape(place_count, heads_kv, DH), 0, 1), repeat, axis=0
        )
        return jnp.concatenate([query_rows, key_rows, value_rows], axis=1)
    rows = queries.shape[1] // DH // heads_kv * place_count + 2 * place_count
    return pl.pallas_call(
        pack_kernel, out_shape=jax.ShapeDtypeStruct((ctx, rows, DH), queries.dtype)
    )(queries, own_keys, own_values)


def right_step(query_grid, block_keys):
    logits = jnp.einsum(
        "lpd,lid->lpi", query_grid, block_keys, preferred_element_type=jnp.float32
    ) / math.sqrt(DH)
    weights, entropy = softmax_terms(logits)
    rounded = weights.astype(jnp.bfloat16)
    key_mix = jnp.einsum(
        "lpi,lid->lpd", rounded, block_keys, preferred_element_type=jnp.float32
    ).astype(jnp.bfloat16)
    return rounded, entropy, key_mix


def one_sequence(queries, own_keys, own_values, ctx):
    place_count, feature_width = queries.shape
    own_len = own_keys.shape[0]
    heads_kv = own_keys.shape[1] // DH
    chunk = feature_width // DH * place_count // ctx
    rows = exchange(pack(queries, own_keys, own_values, ctx))
    query_grid = rows[:, :chunk]
    halves = lax.all_gather(
        rows[:, chunk:].reshape(ctx, 2, own_len, DH), "head", axis=2, tiled=True
    )
    block_keys, block_values = halves[:, 0], halves[:, 1]

    _, entropy_grid, key_grid = right_step(query_grid, block_keys)
    weights, left_rounded = left_step(query_grid, key_grid, entropy_grid)
    column_mass = jnp.sum(weights, axis=0)
    mixed = jnp.einsum(
        "alp,apd->lpd", left_rounded, query_grid, preferred_element_type=jnp.float32
    )
    query_mix = (mixed / jnp.maximum(column_mass, 1.0)[..., None]).astype(jnp.bfloat16)

    rounded, entropy, key_mix = right_step(query_mix, block_keys)
    value_mix = jnp.einsum(
        "lpi,lid->lpd", rounded, block_values, preferred_element_type=jnp.float32
    ).astype(jnp.bfloat16)

    _, final_left = left_step(query_grid, key_mix, entropy)
    attended = jnp.einsum(
        "alp,lpd->apd", final_left, value_mix, preferred_element_type=jnp.float32
    ).astype(jnp.bfloat16)
    return from_dest(exchange(attended), place_count, heads_kv)


def make_local(ctx):
    def local(queries, key_states, value_states):
        return jnp.stack(
            [
                one_sequence(queries[s], key_states[s], value_states[s], ctx)
                for s in range(queries.shape[0])
            ]
        )

    return local


def solution(mesh):
    placed = P("grp", ("ctx", "head"), None)
    return jax.shard_map(
        make_local(mesh.shape["ctx"]),
        mesh=mesh,
        in_specs=(placed, placed, placed),
        out_specs=placed,
        check_vma=False,
    )
```

```python
import math

import jax
import jax.numpy as jnp
from jax import lax
from jax.experimental import pallas as pl
from jax.sharding import PartitionSpec as P

DH = 128


def softmax_terms(logits):
    weights = jax.nn.softmax(logits, axis=-1)
    entropy = jax.nn.logsumexp(logits, axis=-1) - jnp.sum(weights * logits, axis=-1)
    return weights, entropy


def exchange(grid):
    return lax.all_to_all(grid, "ctx", split_axis=0, concat_axis=0, tiled=True)


def left_step(query_grid, key_grid, entropy_grid):
    logits = jnp.einsum(
        "apd,lpd->alp", query_grid, key_grid, preferred_element_type=jnp.float32
    ) / math.sqrt(DH)
    logits = logits + entropy_grid[None]
    weights = jax.nn.softmax(logits, axis=1)
    return weights, weights.astype(jnp.bfloat16)


def to_dest(rows, ctx, heads_kv):
    place_count, group = rows.shape[0], rows.shape[2]
    repeat = ctx // heads_kv
    shaped = rows.reshape((repeat, place_count // repeat) + rows.shape[1:])
    shaped = jnp.moveaxis(shaped, (2, 0, 3), (0, 1, 2))
    return shaped.reshape((ctx, place_count // repeat * group) + rows.shape[3:])


def from_dest(grid, place_count, heads_kv):
    ctx = grid.shape[0]
    repeat = ctx // heads_kv
    shaped = grid.reshape(heads_kv, repeat, -1, place_count // repeat, DH)
    shaped = jnp.moveaxis(shaped, (0, 1, 2), (2, 0, 3))
    return shaped.reshape(place_count, -1)


def pack_kernel(query_ref, key_ref, value_ref, out_ref):
    place_count = query_ref.shape[0]
    group = query_ref.shape[1] // DH
    for g in range(group):
        out_ref[0, g * place_count : (g + 1) * place_count, :] = query_ref[:, g * DH : (g + 1) * DH]
    base = group * place_count
    out_ref[0, base : base + place_count, :] = key_ref[...]
    out_ref[0, base + place_count : base + 2 * place_count, :] = value_ref[...]


def pack(queries, own_keys, own_values, ctx):
    place_count = queries.shape[0]
    heads_kv = own_keys.shape[1] // DH
    if ctx != heads_kv:
        repeat = ctx // heads_kv
        query_rows = to_dest(queries.reshape(place_count, heads_kv, -1, DH), ctx, heads_kv)
        key_rows = jnp.repeat(
            jnp.swapaxes(own_keys.reshape(place_count, heads_kv, DH), 0, 1), repeat, axis=0
        )
        value_rows = jnp.repeat(
            jnp.swapaxes(own_values.reshape(place_count, heads_kv, DH), 0, 1), repeat, axis=0
        )
        return jnp.concatenate([query_rows, key_rows, value_rows], axis=1)
    group = queries.shape[1] // DH // heads_kv
    rows = group * place_count + 2 * place_count
    return pl.pallas_call(
        pack_kernel,
        grid=(ctx,),
        in_specs=[
            pl.BlockSpec((place_count, group * DH), lambda i: (0, i)),
            pl.BlockSpec((place_count, DH), lambda i: (0, i)),
            pl.BlockSpec((place_count, DH), lambda i: (0, i)),
        ],
        out_specs=pl.BlockSpec((1, rows, DH), lambda i: (i, 0, 0)),
        out_shape=jax.ShapeDtypeStruct((ctx, rows, DH), queries.dtype),
    )(queries, own_keys, own_values)


def right_step(query_grid, block_keys):
    logits = jnp.einsum(
        "lpd,lid->lpi", query_grid, block_keys, preferred_element_type=jnp.float32
    ) / math.sqrt(DH)
    weights, entropy = softmax_terms(logits)
    rounded = weights.astype(jnp.bfloat16)
    key_mix = jnp.einsum(
        "lpi,lid->lpd", rounded, block_keys, preferred_element_type=jnp.float32
    ).astype(jnp.bfloat16)
    return rounded, entropy, key_mix


def one_sequence(queries, own_keys, own_values, ctx):
    place_count, feature_width = queries.shape
    own_len = own_keys.shape[0]
    heads_kv = own_keys.shape[1] // DH
    chunk = feature_width // DH * place_count // ctx
    rows = exchange(pack(queries, own_keys, own_values, ctx))
    query_grid = rows[:, :chunk]
    halves = lax.all_gather(
        rows[:, chunk:].reshape(ctx, 2, own_len, DH), "head", axis=2, tiled=True
    )
    block_keys, block_values = halves[:, 0], halves[:, 1]

    _, entropy_grid, key_grid = right_step(query_grid, block_keys)
    weights, left_rounded = left_step(query_grid, key_grid, entropy_grid)
    column_mass = jnp.sum(weights, axis=0)
    mixed = jnp.einsum(
        "alp,apd->lpd", left_rounded, query_grid, preferred_element_type=jnp.float32
    )
    query_mix = (mixed / jnp.maximum(column_mass, 1.0)[..., None]).astype(jnp.bfloat16)

    rounded, entropy, key_mix = right_step(query_mix, block_keys)
    value_mix = jnp.einsum(
        "lpi,lid->lpd", rounded, block_values, preferred_element_type=jnp.float32
    ).astype(jnp.bfloat16)

    _, final_left = left_step(query_grid, key_mix, entropy)
    attended = jnp.einsum(
        "alp,lpd->apd", final_left, value_mix, preferred_element_type=jnp.float32
    ).astype(jnp.bfloat16)
    return from_dest(exchange(attended), place_count, heads_kv)


def make_local(ctx):
    def local(queries, key_states, value_states):
        return jnp.stack(
            [
                one_sequence(queries[s], key_states[s], value_states[s], ctx)
                for s in range(queries.shape[0])
            ]
        )

    return local


def solution(mesh):
    placed = P("grp", ("ctx", "head"), None)
    return jax.shard_map(
        make_local(mesh.shape["ctx"]),
        mesh=mesh,
        in_specs=(placed, placed, placed),
        out_specs=placed,
        check_vma=False,
    )
```

```python
import math

import jax
import jax.numpy as jnp
from jax import lax
from jax.experimental import pallas as pl
from jax.sharding import PartitionSpec as P

DH = 128


def softmax_terms(logits):
    weights = jax.nn.softmax(logits, axis=-1)
    entropy = jax.nn.logsumexp(logits, axis=-1) - jnp.sum(weights * logits, axis=-1)
    return weights, entropy


def exchange(grid):
    return lax.all_to_all(grid, "ctx", split_axis=0, concat_axis=0, tiled=True)


def left_step(query_grid, key_grid, entropy_grid):
    logits = jnp.einsum(
        "apd,lpd->alp", query_grid, key_grid, preferred_element_type=jnp.float32
    ) / math.sqrt(DH)
    logits = logits + entropy_grid[None]
    weights = jax.nn.softmax(logits, axis=1)
    return weights, weights.astype(jnp.bfloat16)


def to_dest(rows, ctx, heads_kv):
    place_count, group = rows.shape[0], rows.shape[2]
    repeat = ctx // heads_kv
    shaped = rows.reshape((repeat, place_count // repeat) + rows.shape[1:])
    shaped = jnp.moveaxis(shaped, (2, 0, 3), (0, 1, 2))
    return shaped.reshape((ctx, place_count // repeat * group) + rows.shape[3:])


def from_dest(grid, place_count, heads_kv):
    ctx = grid.shape[0]
    repeat = ctx // heads_kv
    shaped = grid.reshape(heads_kv, repeat, -1, place_count // repeat, DH)
    shaped = jnp.moveaxis(shaped, (0, 1, 2), (2, 0, 3))
    return shaped.reshape(place_count, -1)


def pack_kernel(query_ref, key_ref, value_ref, out_ref):
    place_count = query_ref.shape[0]
    ctx = out_ref.shape[0]
    group = query_ref.shape[1] // key_ref.shape[1]
    for dest in range(ctx):
        for g in range(group):
            head = dest * group + g
            out_ref[dest, g * place_count : (g + 1) * place_count, :] = query_ref[
                :, head * DH : (head + 1) * DH
            ]
        base = group * place_count
        out_ref[dest, base : base + place_count, :] = key_ref[:, dest * DH : (dest + 1) * DH]
        base += place_count
        out_ref[dest, base : base + place_count, :] = value_ref[:, dest * DH : (dest + 1) * DH]


def pack(queries, own_keys, own_values, ctx):
    place_count = queries.shape[0]
    heads_kv = own_keys.shape[1] // DH
    if ctx != heads_kv:
        repeat = ctx // heads_kv
        query_rows = to_dest(queries.reshape(place_count, heads_kv, -1, DH), ctx, heads_kv)
        key_rows = jnp.repeat(
            jnp.swapaxes(own_keys.reshape(place_count, heads_kv, DH), 0, 1), repeat, axis=0
        )
        value_rows = jnp.repeat(
            jnp.swapaxes(own_values.reshape(place_count, heads_kv, DH), 0, 1), repeat, axis=0
        )
        return jnp.concatenate([query_rows, key_rows, value_rows], axis=1)
    rows = queries.shape[1] // DH // heads_kv * place_count + 2 * place_count
    return pl.pallas_call(
        pack_kernel, out_shape=jax.ShapeDtypeStruct((ctx, rows, DH), queries.dtype)
    )(queries, own_keys, own_values)


def right_step(query_grid, block_keys):
    logits = jnp.einsum(
        "lpd,lid->lpi", query_grid, block_keys, preferred_element_type=jnp.float32
    ) / math.sqrt(DH)
    weights, entropy = softmax_terms(logits)
    rounded = weights.astype(jnp.bfloat16)
    key_mix = jnp.einsum(
        "lpi,lid->lpd", rounded, block_keys, preferred_element_type=jnp.float32
    ).astype(jnp.bfloat16)
    return rounded, entropy, key_mix


def one_sequence(queries, own_keys, own_values, ctx):
    place_count, feature_width = queries.shape
    own_len = own_keys.shape[0]
    heads_kv = own_keys.shape[1] // DH
    chunk = feature_width // DH * place_count // ctx
    rows = exchange(pack(queries, own_keys, own_values, ctx))
    query_grid = rows[:, :chunk]
    halves = lax.all_gather(
        rows[:, chunk:].reshape(ctx, 2, own_len, DH), "head", axis=2, tiled=True
    )
    block_keys, block_values = halves[:, 0], halves[:, 1]

    _, entropy_grid, key_grid = right_step(query_grid, block_keys)
    weights, left_rounded = left_step(query_grid, key_grid, entropy_grid)
    column_mass = jnp.sum(weights, axis=0)
    mixed = jnp.einsum(
        "alp,apd->lpd", left_rounded, query_grid, preferred_element_type=jnp.float32
    )
    query_mix = (mixed / jnp.maximum(column_mass, 1.0)[..., None]).astype(jnp.bfloat16)

    rounded, entropy, key_mix = right_step(query_mix, block_keys)
    value_mix = jnp.einsum(
        "lpi,lid->lpd", rounded, block_values, preferred_element_type=jnp.float32
    ).astype(jnp.bfloat16)

    _, final_left = left_step(query_grid, key_mix, entropy)
    if ctx != heads_kv:
        attended = jnp.einsum(
            "alp,lpd->apd", final_left, value_mix, preferred_element_type=jnp.float32
        ).astype(jnp.bfloat16)
        return from_dest(exchange(attended), place_count, heads_kv)
    blocks, groups = final_left.shape[0], chunk // place_count
    tiles = place_count // 8
    attended = jnp.einsum(
        "algbc,lgbcd->bagcd",
        final_left.reshape(blocks, blocks, groups, tiles, 8),
        value_mix.reshape(blocks, groups, tiles, 8, DH),
        preferred_element_type=jnp.float32,
    ).astype(jnp.bfloat16)
    back = lax.all_to_all(attended, "ctx", split_axis=1, concat_axis=1, tiled=True)
    return jnp.transpose(back, (0, 3, 1, 2, 4)).reshape(place_count, feature_width)


def make_local(ctx):
    def local(queries, key_states, value_states):
        return jnp.stack(
            [
                one_sequence(queries[s], key_states[s], value_states[s], ctx)
                for s in range(queries.shape[0])
            ]
        )

    return local


def solution(mesh):
    placed = P("grp", ("ctx", "head"), None)
    return jax.shard_map(
        make_local(mesh.shape["ctx"]),
        mesh=mesh,
        in_specs=(placed, placed, placed),
        out_specs=placed,
        check_vma=False,
    )
```

```python
import math

import jax
import jax.numpy as jnp
from jax import lax
from jax.experimental import pallas as pl
from jax.sharding import PartitionSpec as P

DH = 128


def softmax_terms(logits):
    weights = jax.nn.softmax(logits, axis=-1)
    entropy = jax.nn.logsumexp(logits, axis=-1) - jnp.sum(weights * logits, axis=-1)
    return weights, entropy


def exchange(grid):
    return lax.all_to_all(grid, "ctx", split_axis=0, concat_axis=0, tiled=True)


def left_step(query_grid, key_grid, entropy_grid):
    logits = jnp.einsum(
        "apd,lpd->alp", query_grid, key_grid, preferred_element_type=jnp.float32
    ) / math.sqrt(DH)
    logits = logits + entropy_grid[None]
    weights = jax.nn.softmax(logits, axis=1)
    return weights, weights.astype(jnp.bfloat16)


def to_dest(rows, ctx, heads_kv):
    place_count, group = rows.shape[0], rows.shape[2]
    repeat = ctx // heads_kv
    shaped = rows.reshape((repeat, place_count // repeat) + rows.shape[1:])
    shaped = jnp.moveaxis(shaped, (2, 0, 3), (0, 1, 2))
    return shaped.reshape((ctx, place_count // repeat * group) + rows.shape[3:])


def from_dest(grid, place_count, heads_kv):
    ctx = grid.shape[0]
    repeat = ctx // heads_kv
    shaped = grid.reshape(heads_kv, repeat, -1, place_count // repeat, DH)
    shaped = jnp.moveaxis(shaped, (0, 1, 2), (2, 0, 3))
    return shaped.reshape(place_count, -1)


def pack_kernel(query_ref, key_ref, value_ref, out_ref):
    place_count = query_ref.shape[0]
    ctx = out_ref.shape[0]
    group = query_ref.shape[1] // key_ref.shape[1]
    for dest in range(ctx):
        for g in range(group):
            head = dest * group + g
            out_ref[dest, g * place_count : (g + 1) * place_count, :] = query_ref[
                :, head * DH : (head + 1) * DH
            ]
        base = group * place_count
        out_ref[dest, base : base + place_count, :] = key_ref[:, dest * DH : (dest + 1) * DH]
        base += place_count
        out_ref[dest, base : base + place_count, :] = value_ref[:, dest * DH : (dest + 1) * DH]


def pack(queries, own_keys, own_values, ctx):
    place_count = queries.shape[0]
    heads_kv = own_keys.shape[1] // DH
    if ctx != heads_kv:
        repeat = ctx // heads_kv
        query_rows = to_dest(queries.reshape(place_count, heads_kv, -1, DH), ctx, heads_kv)
        key_rows = jnp.repeat(
            jnp.swapaxes(own_keys.reshape(place_count, heads_kv, DH), 0, 1), repeat, axis=0
        )
        value_rows = jnp.repeat(
            jnp.swapaxes(own_values.reshape(place_count, heads_kv, DH), 0, 1), repeat, axis=0
        )
        return jnp.concatenate([query_rows, key_rows, value_rows], axis=1)
    rows = queries.shape[1] // DH // heads_kv * place_count + 2 * place_count
    return pl.pallas_call(
        pack_kernel, out_shape=jax.ShapeDtypeStruct((ctx, rows, DH), queries.dtype)
    )(queries, own_keys, own_values)


def right_step(query_grid, block_keys):
    logits = jnp.einsum(
        "lpd,lid->lpi", query_grid, block_keys, preferred_element_type=jnp.float32
    ) / math.sqrt(DH)
    weights, entropy = softmax_terms(logits)
    rounded = weights.astype(jnp.bfloat16)
    key_mix = jnp.einsum(
        "lpi,lid->lpd", rounded, block_keys, preferred_element_type=jnp.float32
    ).astype(jnp.bfloat16)
    return rounded, entropy, key_mix


def one_sequence(queries, own_keys, own_values, ctx):
    place_count, feature_width = queries.shape
    own_len = own_keys.shape[0]
    heads_kv = own_keys.shape[1] // DH
    chunk = feature_width // DH * place_count // ctx
    rows = exchange(pack(queries, own_keys, own_values, ctx))
    query_grid = rows[:, :chunk]
    halves = lax.all_gather(
        rows[:, chunk:].reshape(ctx, 2, own_len, DH), "head", axis=2, tiled=True
    )
    block_keys, block_values = halves[:, 0], halves[:, 1]

    _, entropy_grid, key_grid = right_step(query_grid, block_keys)
    weights, left_rounded = left_step(query_grid, key_grid, entropy_grid)
    column_mass = jnp.sum(weights, axis=0)
    mixed = jnp.einsum(
        "alp,apd->lpd", left_rounded, query_grid, preferred_element_type=jnp.float32
    )
    query_mix = (mixed / jnp.maximum(column_mass, 1.0)[..., None]).astype(jnp.bfloat16)

    rounded, entropy, key_mix = right_step(query_mix, block_keys)
    value_mix = jnp.einsum(
        "lpi,lid->lpd", rounded, block_values, preferred_element_type=jnp.float32
    ).astype(jnp.bfloat16)

    _, final_left = left_step(query_grid, key_mix, entropy)
    if ctx != heads_kv:
        attended = jnp.einsum(
            "alp,lpd->apd", final_left, value_mix, preferred_element_type=jnp.float32
        ).astype(jnp.bfloat16)
        return from_dest(exchange(attended), place_count, heads_kv)
    blocks, groups = final_left.shape[0], chunk // place_count
    tiles = place_count // 8
    attended = jnp.einsum(
        "algbc,lgbcd->bcagd",
        final_left.reshape(blocks, blocks, groups, tiles, 8),
        value_mix.reshape(blocks, groups, tiles, 8, DH),
        preferred_element_type=jnp.float32,
    ).astype(jnp.bfloat16)
    back = lax.all_to_all(attended, "ctx", split_axis=2, concat_axis=2, tiled=True)
    return back.reshape(place_count, feature_width)


def make_local(ctx):
    def local(queries, key_states, value_states):
        return jnp.stack(
            [
                one_sequence(queries[s], key_states[s], value_states[s], ctx)
                for s in range(queries.shape[0])
            ]
        )

    return local


def solution(mesh):
    placed = P("grp", ("ctx", "head"), None)
    return jax.shard_map(
        make_local(mesh.shape["ctx"]),
        mesh=mesh,
        in_specs=(placed, placed, placed),
        out_specs=placed,
        check_vma=False,
    )
```

```python
import math

import jax
import jax.numpy as jnp
from jax import lax
from jax.experimental import pallas as pl
from jax.sharding import PartitionSpec as P

DH = 128


def softmax_terms(logits):
    weights = jax.nn.softmax(logits, axis=-1)
    entropy = jax.nn.logsumexp(logits, axis=-1) - jnp.sum(weights * logits, axis=-1)
    return weights, entropy


def exchange(grid):
    return lax.all_to_all(grid, "ctx", split_axis=0, concat_axis=0, tiled=True)


def left_step(query_grid, key_grid, entropy_grid):
    logits = jnp.einsum(
        "apd,lpd->alp", query_grid, key_grid, preferred_element_type=jnp.float32
    ) / math.sqrt(DH)
    logits = logits + entropy_grid[None]
    weights = jax.nn.softmax(logits, axis=1)
    return weights, weights.astype(jnp.bfloat16)


def to_dest(rows, ctx, heads_kv):
    place_count, group = rows.shape[0], rows.shape[2]
    repeat = ctx // heads_kv
    shaped = rows.reshape((repeat, place_count // repeat) + rows.shape[1:])
    shaped = jnp.moveaxis(shaped, (2, 0, 3), (0, 1, 2))
    return shaped.reshape((ctx, place_count // repeat * group) + rows.shape[3:])


def from_dest(grid, place_count, heads_kv):
    ctx = grid.shape[0]
    repeat = ctx // heads_kv
    shaped = grid.reshape(heads_kv, repeat, -1, place_count // repeat, DH)
    shaped = jnp.moveaxis(shaped, (0, 1, 2), (2, 0, 3))
    return shaped.reshape(place_count, -1)


def pack_kernel(query_ref, key_ref, value_ref, out_ref):
    place_count = query_ref.shape[0]
    ctx = out_ref.shape[0]
    group = query_ref.shape[1] // key_ref.shape[1]
    for dest in range(ctx):
        for g in range(group):
            head = dest * group + g
            out_ref[dest, g * place_count : (g + 1) * place_count, :] = query_ref[
                :, head * DH : (head + 1) * DH
            ]
        base = group * place_count
        out_ref[dest, base : base + place_count, :] = key_ref[:, dest * DH : (dest + 1) * DH]
        base += place_count
        out_ref[dest, base : base + place_count, :] = value_ref[:, dest * DH : (dest + 1) * DH]


def pack(queries, own_keys, own_values, ctx):
    place_count = queries.shape[0]
    heads_kv = own_keys.shape[1] // DH
    if ctx != heads_kv:
        repeat = ctx // heads_kv
        query_rows = to_dest(queries.reshape(place_count, heads_kv, -1, DH), ctx, heads_kv)
        key_rows = jnp.repeat(
            jnp.swapaxes(own_keys.reshape(place_count, heads_kv, DH), 0, 1), repeat, axis=0
        )
        value_rows = jnp.repeat(
            jnp.swapaxes(own_values.reshape(place_count, heads_kv, DH), 0, 1), repeat, axis=0
        )
        return jnp.concatenate([query_rows, key_rows, value_rows], axis=1)
    rows = queries.shape[1] // DH // heads_kv * place_count + 2 * place_count
    return pl.pallas_call(
        pack_kernel, out_shape=jax.ShapeDtypeStruct((ctx, rows, DH), queries.dtype)
    )(queries, own_keys, own_values)


def right_step(query_grid, block_keys):
    logits = jnp.einsum(
        "lpd,lid->lpi", query_grid, block_keys, preferred_element_type=jnp.float32
    ) / math.sqrt(DH)
    weights, entropy = softmax_terms(logits)
    rounded = weights.astype(jnp.bfloat16)
    key_mix = jnp.einsum(
        "lpi,lid->lpd", rounded, block_keys, preferred_element_type=jnp.float32
    ).astype(jnp.bfloat16)
    return rounded, entropy, key_mix


def one_sequence(queries, own_keys, own_values, ctx):
    place_count, feature_width = queries.shape
    own_len = own_keys.shape[0]
    heads_kv = own_keys.shape[1] // DH
    chunk = feature_width // DH * place_count // ctx
    rows = exchange(pack(queries, own_keys, own_values, ctx))
    query_grid = rows[:, :chunk]
    halves = lax.all_gather(
        rows[:, chunk:].reshape(ctx, 2, own_len, DH), "head", axis=2, tiled=True
    )
    block_keys, block_values = halves[:, 0], halves[:, 1]

    _, entropy_grid, key_grid = right_step(query_grid, block_keys)
    weights, left_rounded = left_step(query_grid, key_grid, entropy_grid)
    column_mass = jnp.sum(weights, axis=0)
    if ctx != heads_kv:
        mixed = jnp.einsum(
            "alp,apd->lpd", left_rounded, query_grid, preferred_element_type=jnp.float32
        )
    else:
        blocks, groups = left_rounded.shape[0], chunk // place_count
        mixed = jnp.einsum(
            "algbc,agbcd->lgbcd",
            left_rounded.reshape(blocks, blocks, groups, place_count // 8, 8),
            query_grid.reshape(blocks, groups, place_count // 8, 8, DH),
            preferred_element_type=jnp.float32,
        ).reshape(blocks, chunk, DH)
    query_mix = (mixed / jnp.maximum(column_mass, 1.0)[..., None]).astype(jnp.bfloat16)

    rounded, entropy, key_mix = right_step(query_mix, block_keys)
    value_mix = jnp.einsum(
        "lpi,lid->lpd", rounded, block_values, preferred_element_type=jnp.float32
    ).astype(jnp.bfloat16)

    _, final_left = left_step(query_grid, key_mix, entropy)
    if ctx != heads_kv:
        attended = jnp.einsum(
            "alp,lpd->apd", final_left, value_mix, preferred_element_type=jnp.float32
        ).astype(jnp.bfloat16)
        return from_dest(exchange(attended), place_count, heads_kv)
    blocks, groups = final_left.shape[0], chunk // place_count
    tiles = place_count // 8
    attended = jnp.einsum(
        "algbc,lgbcd->bagcd",
        final_left.reshape(blocks, blocks, groups, tiles, 8),
        value_mix.reshape(blocks, groups, tiles, 8, DH),
        preferred_element_type=jnp.float32,
    ).astype(jnp.bfloat16)
    back = lax.all_to_all(attended, "ctx", split_axis=1, concat_axis=1, tiled=True)
    return jnp.transpose(back, (0, 3, 1, 2, 4)).reshape(place_count, feature_width)


def make_local(ctx):
    def local(queries, key_states, value_states):
        return jnp.stack(
            [
                one_sequence(queries[s], key_states[s], value_states[s], ctx)
                for s in range(queries.shape[0])
            ]
        )

    return local


def solution(mesh):
    placed = P("grp", ("ctx", "head"), None)
    return jax.shard_map(
        make_local(mesh.shape["ctx"]),
        mesh=mesh,
        in_specs=(placed, placed, placed),
        out_specs=placed,
        check_vma=False,
    )
```

```python
import math

import jax
import jax.numpy as jnp
from jax import lax
from jax.experimental import pallas as pl
from jax.sharding import PartitionSpec as P

DH = 128


def softmax_terms(logits):
    weights = jax.nn.softmax(logits, axis=-1)
    entropy = jax.nn.logsumexp(logits, axis=-1) - jnp.sum(weights * logits, axis=-1)
    return weights, entropy


def exchange(grid):
    return lax.all_to_all(grid, "ctx", split_axis=0, concat_axis=0, tiled=True)


def left_step(query_grid, key_grid, entropy_grid):
    blocks, pairs, _ = query_grid.shape
    if pairs % 32:
        logits = jnp.einsum(
            "apd,lpd->alp", query_grid, key_grid, preferred_element_type=jnp.float32
        )
    else:
        logits = jnp.einsum(
            "agbcd,lgbcd->algbc",
            query_grid.reshape(blocks, 4, -1, 8, DH),
            key_grid.reshape(blocks, 4, -1, 8, DH),
            preferred_element_type=jnp.float32,
        ).reshape(blocks, blocks, pairs)
    logits = logits / math.sqrt(DH) + entropy_grid[None]
    weights = jax.nn.softmax(logits, axis=1)
    return weights, weights.astype(jnp.bfloat16)


def to_dest(rows, ctx, heads_kv):
    place_count, group = rows.shape[0], rows.shape[2]
    repeat = ctx // heads_kv
    shaped = rows.reshape((repeat, place_count // repeat) + rows.shape[1:])
    shaped = jnp.moveaxis(shaped, (2, 0, 3), (0, 1, 2))
    return shaped.reshape((ctx, place_count // repeat * group) + rows.shape[3:])


def from_dest(grid, place_count, heads_kv):
    ctx = grid.shape[0]
    repeat = ctx // heads_kv
    shaped = grid.reshape(heads_kv, repeat, -1, place_count // repeat, DH)
    shaped = jnp.moveaxis(shaped, (0, 1, 2), (2, 0, 3))
    return shaped.reshape(place_count, -1)


def pack_kernel(query_ref, key_ref, value_ref, out_ref):
    place_count = query_ref.shape[0]
    ctx = out_ref.shape[0]
    group = query_ref.shape[1] // key_ref.shape[1]
    for dest in range(ctx):
        for g in range(group):
            head = dest * group + g
            out_ref[dest, g * place_count : (g + 1) * place_count, :] = query_ref[
                :, head * DH : (head + 1) * DH
            ]
        base = group * place_count
        out_ref[dest, base : base + place_count, :] = key_ref[:, dest * DH : (dest + 1) * DH]
        base += place_count
        out_ref[dest, base : base + place_count, :] = value_ref[:, dest * DH : (dest + 1) * DH]


def pack(queries, own_keys, own_values, ctx):
    place_count = queries.shape[0]
    heads_kv = own_keys.shape[1] // DH
    if ctx != heads_kv:
        repeat = ctx // heads_kv
        query_rows = to_dest(queries.reshape(place_count, heads_kv, -1, DH), ctx, heads_kv)
        key_rows = jnp.repeat(
            jnp.swapaxes(own_keys.reshape(place_count, heads_kv, DH), 0, 1), repeat, axis=0
        )
        value_rows = jnp.repeat(
            jnp.swapaxes(own_values.reshape(place_count, heads_kv, DH), 0, 1), repeat, axis=0
        )
        return jnp.concatenate([query_rows, key_rows, value_rows], axis=1)
    rows = queries.shape[1] // DH // heads_kv * place_count + 2 * place_count
    return pl.pallas_call(
        pack_kernel, out_shape=jax.ShapeDtypeStruct((ctx, rows, DH), queries.dtype)
    )(queries, own_keys, own_values)


def right_step(query_grid, block_keys):
    logits = jnp.einsum(
        "lpd,lid->lpi", query_grid, block_keys, preferred_element_type=jnp.float32
    ) / math.sqrt(DH)
    weights, entropy = softmax_terms(logits)
    rounded = weights.astype(jnp.bfloat16)
    key_mix = jnp.einsum(
        "lpi,lid->lpd", rounded, block_keys, preferred_element_type=jnp.float32
    ).astype(jnp.bfloat16)
    return rounded, entropy, key_mix


def one_sequence(queries, own_keys, own_values, ctx):
    place_count, feature_width = queries.shape
    own_len = own_keys.shape[0]
    heads_kv = own_keys.shape[1] // DH
    chunk = feature_width // DH * place_count // ctx
    rows = exchange(pack(queries, own_keys, own_values, ctx))
    query_grid = rows[:, :chunk]
    halves = lax.all_gather(
        rows[:, chunk:].reshape(ctx, 2, own_len, DH), "head", axis=2, tiled=True
    )
    block_keys, block_values = halves[:, 0], halves[:, 1]

    _, entropy_grid, key_grid = right_step(query_grid, block_keys)
    weights, left_rounded = left_step(query_grid, key_grid, entropy_grid)
    column_mass = jnp.sum(weights, axis=0)
    mixed = jnp.einsum(
        "alp,apd->lpd", left_rounded, query_grid, preferred_element_type=jnp.float32
    )
    query_mix = (mixed / jnp.maximum(column_mass, 1.0)[..., None]).astype(jnp.bfloat16)

    rounded, entropy, key_mix = right_step(query_mix, block_keys)
    value_mix = jnp.einsum(
        "lpi,lid->lpd", rounded, block_values, preferred_element_type=jnp.float32
    ).astype(jnp.bfloat16)

    _, final_left = left_step(query_grid, key_mix, entropy)
    if ctx != heads_kv:
        attended = jnp.einsum(
            "alp,lpd->apd", final_left, value_mix, preferred_element_type=jnp.float32
        ).astype(jnp.bfloat16)
        return from_dest(exchange(attended), place_count, heads_kv)
    blocks, groups = final_left.shape[0], chunk // place_count
    tiles = place_count // 8
    attended = jnp.einsum(
        "algbc,lgbcd->bagcd",
        final_left.reshape(blocks, blocks, groups, tiles, 8),
        value_mix.reshape(blocks, groups, tiles, 8, DH),
        preferred_element_type=jnp.float32,
    ).astype(jnp.bfloat16)
    back = lax.all_to_all(attended, "ctx", split_axis=1, concat_axis=1, tiled=True)
    return jnp.transpose(back, (0, 3, 1, 2, 4)).reshape(place_count, feature_width)


def make_local(ctx):
    def local(queries, key_states, value_states):
        return jnp.stack(
            [
                one_sequence(queries[s], key_states[s], value_states[s], ctx)
                for s in range(queries.shape[0])
            ]
        )

    return local


def solution(mesh):
    placed = P("grp", ("ctx", "head"), None)
    return jax.shard_map(
        make_local(mesh.shape["ctx"]),
        mesh=mesh,
        in_specs=(placed, placed, placed),
        out_specs=placed,
        check_vma=False,
    )
```

```python
import math

import jax
import jax.numpy as jnp
from jax import lax
from jax.experimental import pallas as pl
from jax.sharding import PartitionSpec as P

DH = 128


def softmax_terms(logits):
    weights = jax.nn.softmax(logits, axis=-1)
    entropy = jax.nn.logsumexp(logits, axis=-1) - jnp.sum(weights * logits, axis=-1)
    return weights, entropy


def exchange(grid):
    return lax.all_to_all(grid, "ctx", split_axis=0, concat_axis=0, tiled=True)


def left_step(query_grid, key_grid, entropy_grid):
    logits = jnp.einsum(
        "apd,lpd->alp", query_grid, key_grid, preferred_element_type=jnp.float32
    ) / math.sqrt(DH)
    logits = logits + entropy_grid[None]
    weights = jax.nn.softmax(logits, axis=1)
    return weights, weights.astype(jnp.bfloat16)


def to_dest(rows, ctx, heads_kv):
    place_count, group = rows.shape[0], rows.shape[2]
    repeat = ctx // heads_kv
    shaped = rows.reshape((repeat, place_count // repeat) + rows.shape[1:])
    shaped = jnp.moveaxis(shaped, (2, 0, 3), (0, 1, 2))
    return shaped.reshape((ctx, place_count // repeat * group) + rows.shape[3:])


def from_dest(grid, place_count, heads_kv):
    ctx = grid.shape[0]
    repeat = ctx // heads_kv
    shaped = grid.reshape(heads_kv, repeat, -1, place_count // repeat, DH)
    shaped = jnp.moveaxis(shaped, (0, 1, 2), (2, 0, 3))
    return shaped.reshape(place_count, -1)


def pack_kernel(query_ref, key_ref, value_ref, out_ref):
    place_count = query_ref.shape[0]
    ctx = out_ref.shape[0]
    group = query_ref.shape[1] // key_ref.shape[1]
    for dest in range(ctx):
        for g in range(group):
            head = dest * group + g
            out_ref[dest, g * place_count : (g + 1) * place_count, :] = query_ref[
                :, head * DH : (head + 1) * DH
            ]
        base = group * place_count
        out_ref[dest, base : base + place_count, :] = key_ref[:, dest * DH : (dest + 1) * DH]
        base += place_count
        out_ref[dest, base : base + place_count, :] = value_ref[:, dest * DH : (dest + 1) * DH]


def pack(queries, own_keys, own_values, ctx):
    place_count = queries.shape[0]
    heads_kv = own_keys.shape[1] // DH
    if ctx != heads_kv:
        repeat = ctx // heads_kv
        query_rows = to_dest(queries.reshape(place_count, heads_kv, -1, DH), ctx, heads_kv)
        key_rows = jnp.repeat(
            jnp.swapaxes(own_keys.reshape(place_count, heads_kv, DH), 0, 1), repeat, axis=0
        )
        value_rows = jnp.repeat(
            jnp.swapaxes(own_values.reshape(place_count, heads_kv, DH), 0, 1), repeat, axis=0
        )
        return jnp.concatenate([query_rows, key_rows, value_rows], axis=1)
    rows = queries.shape[1] // DH // heads_kv * place_count + 2 * place_count
    return pl.pallas_call(
        pack_kernel, out_shape=jax.ShapeDtypeStruct((ctx, rows, DH), queries.dtype)
    )(queries, own_keys, own_values)


def right_step(query_grid, block_keys):
    logits = jnp.einsum(
        "lpd,lid->lpi", query_grid, block_keys, preferred_element_type=jnp.float32
    ) / math.sqrt(DH)
    weights, entropy = softmax_terms(logits)
    rounded = weights.astype(jnp.bfloat16)
    key_mix = jnp.einsum(
        "lpi,lid->lpd", rounded, block_keys, preferred_element_type=jnp.float32
    ).astype(jnp.bfloat16)
    return rounded, entropy, key_mix


def one_sequence(queries, own_keys, own_values, ctx):
    place_count, feature_width = queries.shape
    own_len = own_keys.shape[0]
    heads_kv = own_keys.shape[1] // DH
    chunk = feature_width // DH * place_count // ctx
    rows = exchange(pack(queries, own_keys, own_values, ctx))
    query_grid = rows[:, :chunk]
    halves = lax.all_gather(
        rows[:, chunk:].reshape(ctx, 2, own_len, DH), "head", axis=2, tiled=True
    )
    block_keys, block_values = halves[:, 0], halves[:, 1]

    _, entropy_grid, key_grid = right_step(query_grid, block_keys)
    weights, left_rounded = left_step(query_grid, key_grid, entropy_grid)
    column_mass = jnp.sum(weights, axis=0)
    mixed = jnp.einsum(
        "alp,apd->lpd", left_rounded, query_grid, preferred_element_type=jnp.float32
    )
    query_mix = (mixed / jnp.maximum(column_mass, 1.0)[..., None]).astype(jnp.bfloat16)

    logits = jnp.einsum(
        "lpd,lid->lpi", query_mix, block_keys, preferred_element_type=jnp.float32
    ) / math.sqrt(DH)
    weights, entropy = softmax_terms(logits)
    both = jnp.concatenate([block_keys, block_values], axis=2)
    mixes = jnp.einsum(
        "lpi,lid->lpd", weights.astype(jnp.bfloat16), both, preferred_element_type=jnp.float32
    ).astype(jnp.bfloat16)
    key_mix, value_mix = mixes[:, :, :DH], mixes[:, :, DH:]

    _, final_left = left_step(query_grid, key_mix, entropy)
    if ctx != heads_kv:
        attended = jnp.einsum(
            "alp,lpd->apd", final_left, value_mix, preferred_element_type=jnp.float32
        ).astype(jnp.bfloat16)
        return from_dest(exchange(attended), place_count, heads_kv)
    blocks, groups = final_left.shape[0], chunk // place_count
    tiles = place_count // 8
    attended = jnp.einsum(
        "algbc,lgbcd->bagcd",
        final_left.reshape(blocks, blocks, groups, tiles, 8),
        value_mix.reshape(blocks, groups, tiles, 8, DH),
        preferred_element_type=jnp.float32,
    ).astype(jnp.bfloat16)
    back = lax.all_to_all(attended, "ctx", split_axis=1, concat_axis=1, tiled=True)
    return jnp.transpose(back, (0, 3, 1, 2, 4)).reshape(place_count, feature_width)


def make_local(ctx):
    def local(queries, key_states, value_states):
        return jnp.stack(
            [
                one_sequence(queries[s], key_states[s], value_states[s], ctx)
                for s in range(queries.shape[0])
            ]
        )

    return local


def solution(mesh):
    placed = P("grp", ("ctx", "head"), None)
    return jax.shard_map(
        make_local(mesh.shape["ctx"]),
        mesh=mesh,
        in_specs=(placed, placed, placed),
        out_specs=placed,
        check_vma=False,
    )
```
